768 devices in a mesh: dp: 64 (over x, y, core), mp: 12 (over z).
Axes of the slice: x: 4, y: 8, z: 12, core: 2. Of those that a mesh axis runs over, the one named last changes fastest.
Arguments:
- hidden: bfloat16 [2, 4096, 4224], P(None, 'dp'), may hold values from 0 to 6, as said below
- proj_weight: bfloat16 [4224, 4224], P(None, 'mp'), may hold values from -0.09375 to 0.09375
Outputs:
- grad_first: bfloat16 [4096, 4224], P('dp', 'mp')
The draws below stay inside these ranges and needn't reach their ends.
Inputs may be any that keep to these rules, and one draw needn't show every extreme that they name: `hidden`: rectified features of 4096 images in two views.
All inputs are finite; a program needn't handle non-finite values.
Results may differ from the reference program's by a relative error of at most 0.0057.
Values may be sent and summed in bfloat16 or wider, within the bound.
No kernel may reach another device: no remote copies, remote signals or barrier semaphores. Data moves between devices by JAX's collectives and lax.ppermute only.
A program may use at most 32 MiB of HBM per device.

```python
import jax
import jax.numpy as jnp
from jax import lax

HID = 4224
PROJ = 4224
IMAGES = 4096


def draw_hidden(key, part):
    keys = jax.random.split(jax.random.fold_in(key, 11), 4)
    base = jax.random.normal(keys[0], (1, IMAGES, HID), jnp.float32)
    noise = 0.5 * jax.random.normal(keys[1], (2, IMAGES, HID), jnp.float32)
    factor = jax.random.normal(keys[2], (1, IMAGES, 1), jnp.float32)
    loading = jax.random.normal(keys[3], (1, 1, HID), jnp.float32)
    pre = base + noise + 0.3 * factor * loading
    return jnp.clip(pre, 0.0, 6.0).astype(jnp.bfloat16)


def steps_of(key, extent, cuts, least, high):
    level = 1.0
    for axis_at, parts in cuts:
        heights = jax.random.uniform(jax.random.fold_in(jax.random.fold_in(key, 6), axis_at), (parts,), jnp.float32, least / len(cuts), high / len(cuts))
        level = level * jnp.repeat(jnp.exp(heights), extent[axis_at] // parts).reshape((-1,) + (1,) * (len(extent) - 1 - axis_at))
    return level


def gaussian(rng, shape, spread, bound, shards=(), kind=jnp.bfloat16):
    entries = jax.random.normal(rng, shape, jnp.float32) * spread
    if len(shards) > 0:
        entries = steps_of(rng, shape, shards, -0.22, 0.18) * entries
    return jnp.clip(entries, min=-bound, max=bound).astype(kind)


def setup_inputs(seed: int = 0) -> dict:
    arg_keys = jax.random.split(jax.random.key(seed), 3)
    hidden = draw_hidden(jax.random.fold_in(arg_keys[2], 71), 0)
    proj_weight = gaussian(arg_keys[1], (HID, PROJ), HID ** -0.5, 0.09375, ((1, 12),))
    return {"hidden": hidden, "proj_weight": proj_weight}


off_weight = 0.0051
eps = 1e-05

def reference(hidden, proj_weight):
    normed = []
    scales = []
    for view in range(2):
        feats = jnp.dot(hidden[view], proj_weight, preferred_element_type=jnp.float32)
        mean = lax.optimization_barrier(jnp.sum(feats, axis=0, keepdims=True)) / IMAGES
        centered = feats - mean
        var = lax.optimization_barrier(jnp.sum(centered * centered, axis=0, keepdims=True)) / IMAGES
        normed.append((centered / jnp.sqrt(var + eps)).astype(jnp.bfloat16))
        scales.append(1.0 / jnp.sqrt(var + eps))
    first, second = (normed[0], normed[1])
    corr = jnp.dot(first.T, second, preferred_element_type=jnp.float32) / IMAGES
    ident = jnp.arange(PROJ, dtype=jnp.int32)[:, None] == jnp.arange(PROJ, dtype=jnp.int32)[None, :]
    grad_corr = jnp.where(ident, 2.0 * (corr - 1.0), 2.0 * off_weight * corr).astype(jnp.bfloat16)
    grad_wide = grad_corr.astype(jnp.float32)
    diag_val = jnp.diagonal(grad_wide)
    scale_sum = (lax.optimization_barrier(jnp.sum(grad_wide * grad_wide, axis=1)) - diag_val * diag_val) / (2.0 * off_weight) + diag_val * (1.0 + diag_val / 2.0)
    back = jnp.dot(second, grad_corr.T, preferred_element_type=jnp.float32)
    result = (back - first.astype(jnp.float32) * scale_sum[None, :]) * scales[0]
    return result.astype(jnp.bfloat16)
```

```python
import jax
import jax.numpy as jnp
from jax import lax
from jax.sharding import Mesh
from jax.sharding import PartitionSpec as P

off_weight = 0.0051
eps = 1e-05
DP = ("x", "y", "c")


def dp_sum(v):
    v = lax.psum(v, "c")
    v = lax.psum(v, "y")
    return lax.psum(v, "x")


def shards(hidden, proj_weight):
    mp_index = lax.axis_index("mp")
    dp_index = lax.axis_index(DP)
    dp_count = lax.axis_size(DP)
    rows = proj_weight.shape[1]
    total = hidden.shape[1] * dp_count
    feats = jnp.einsum("vbh,hc->vbc", hidden, proj_weight, preferred_element_type=jnp.float32)
    sums = dp_sum(jnp.sum(feats, axis=1, keepdims=True))
    mean = sums / total
    centered = feats - mean
    var = dp_sum(jnp.sum(centered * centered, axis=1, keepdims=True)) / total
    normed = (centered / jnp.sqrt(var + eps)).astype(jnp.bfloat16)
    inv_std = 1.0 / jnp.sqrt(var + eps)
    first = normed[0]
    second = normed[1]
    second_full = lax.all_gather(second, "mp", axis=1, tiled=True)
    width = second_full.shape[1] // dp_count
    columns = lax.all_to_all(second_full, DP, split_axis=1, concat_axis=0, tiled=True)
    corr = (
        jnp.einsum(
            "bi,bj->ij",
            lax.all_gather(first, DP, axis=0, tiled=True),
            columns,
            preferred_element_type=jnp.float32,
        )
        / total
    )
    row_ids = mp_index * rows + lax.iota(jnp.int32, rows)[:, None]
    col_ids = dp_index * width + lax.iota(jnp.int32, width)[None, :]
    grad_block = jnp.where(row_ids == col_ids, 2.0 * (corr - 1.0), 2.0 * off_weight * corr).astype(
        jnp.bfloat16
    )
    grad_rows = lax.all_gather(grad_block, DP, axis=1, tiled=True)
    grad_wide = grad_rows.astype(jnp.float32)
    all_cols = lax.iota(jnp.int32, grad_rows.shape[1])[None, :]
    diag_val = jnp.sum(jnp.where(all_cols == row_ids, grad_wide, 0.0), axis=1)
    scale_sum = (jnp.sum(grad_wide * grad_wide, axis=1) - diag_val * diag_val) / (
        2.0 * off_weight
    ) + diag_val * (1.0 + diag_val / 2.0)
    back = jnp.einsum("bj,ij->bi", second_full, grad_rows, preferred_element_type=jnp.float32)
    result = (back - first.astype(jnp.float32) * scale_sum[None, :]) * inv_std[0]
    return result.astype(jnp.bfloat16)


def solution(mesh):
    x, y, c = (4, 8, 2)
    sub = Mesh(mesh.devices.reshape(x, y, c, mesh.devices.shape[1]), DP + ("mp",))
    return jax.shard_map(
        shards,
        mesh=sub,
        in_specs=(P(None, DP, None), P(None, "mp")),
        out_specs=P(DP, "mp"),
        check_vma=False,
    )
```

```python
import jax
import jax.numpy as jnp
from jax import lax
from jax.sharding import Mesh
from jax.sharding import PartitionSpec as P

off_weight = 0.0051
eps = 1e-05
DP = ("x", "y", "c")


def dp_sum(v):
    v = lax.psum(v, "c")
    v = lax.psum(v, "y")
    return lax.psum(v, "x")


def dp_gather(v):
    v = lax.all_gather(v, "x", axis=0)
    v = lax.all_gather(v, "y", axis=0)
    return lax.all_gather(v, "c", axis=0)


def shards(hidden, proj_weight):
    mp_index = lax.axis_index("mp")
    dp_index = lax.axis_index(DP)
    dp_count = lax.axis_size(DP)
    nx, ny, nc = lax.axis_size("x"), lax.axis_size("y"), lax.axis_size("c")
    rows = proj_weight.shape[1]
    local = hidden.shape[1]
    total = local * dp_count
    feats = jnp.einsum("vbh,hc->vbc", hidden, proj_weight, preferred_element_type=jnp.float32)
    sums = dp_sum(jnp.sum(feats, axis=1, keepdims=True))
    mean = sums / total
    centered = feats - mean
    var = dp_sum(jnp.sum(centered * centered, axis=1, keepdims=True)) / total
    normed = (centered / jnp.sqrt(var + eps)).astype(jnp.bfloat16)
    inv_std = 1.0 / jnp.sqrt(var + eps)
    first = normed[0]
    second = normed[1]
    n_mp = lax.axis_size("mp")
    stacked = lax.all_gather(second, "mp", axis=0)
    second_full = jnp.transpose(stacked, (1, 0, 2)).reshape(local, n_mp * rows)
    width = second_full.shape[1] // dp_count
    columns = lax.all_to_all(second_full, DP, split_axis=1, concat_axis=0, tiled=True)
    first_all = dp_gather(first)
    first_all = jnp.transpose(first_all, (2, 1, 0, 3, 4)).reshape(total, rows)
    corr = (
        jnp.einsum("bi,bj->ij", first_all, columns, preferred_element_type=jnp.float32)
        / total
    )
    row_ids = mp_index * rows + lax.iota(jnp.int32, rows)[:, None]
    col_ids = dp_index * width + lax.iota(jnp.int32, width)[None, :]
    grad_block = jnp.where(row_ids == col_ids, 2.0 * (corr - 1.0), 2.0 * off_weight * corr).astype(
        jnp.bfloat16
    )
    grad_t = dp_gather(grad_block.T).reshape(dp_count * width, rows)
    t = lax.iota(jnp.int32, width)
    cc = lax.iota(jnp.int32, nc)[:, None, None, None]
    yy = lax.iota(jnp.int32, ny)[None, :, None, None]
    xx = lax.iota(jnp.int32, nx)[None, None, :, None]
    perm_cols = (((xx * ny + yy) * nc + cc) * width + t[None, None, None, :]).reshape(-1)
    grad_wide = grad_t.astype(jnp.float32)
    row_flat = mp_index * rows + lax.iota(jnp.int32, rows)
    diag_val = jnp.sum(jnp.where(perm_cols[:, None] == row_flat[None, :], grad_wide, 0.0), axis=0)
    scale_sum = (jnp.sum(grad_wide * grad_wide, axis=0) - diag_val * diag_val) / (
        2.0 * off_weight
    ) + diag_val * (1.0 + diag_val / 2.0)
    second_perm = second_full.reshape(local, nx, ny, nc, width)
    second_perm = jnp.transpose(second_perm, (0, 3, 2, 1, 4)).reshape(local, dp_count * width)
    back = jnp.dot(second_perm, grad_t, preferred_element_type=jnp.float32)
    result = (back - first.astype(jnp.float32) * scale_sum[None, :]) * inv_std[0]
    return result.astype(jnp.bfloat16)


def solution(mesh):
    x, y, c = (4, 8, 2)
    sub = Mesh(mesh.devices.reshape(x, y, c, mesh.devices.shape[1]), DP + ("mp",))
    return jax.shard_map(
        shards,
        mesh=sub,
        in_specs=(P(None, DP, None), P(None, "mp")),
        out_specs=P(DP, "mp"),
        check_vma=False,
    )
```

```python
import jax
import jax.numpy as jnp
from jax import lax
from jax.sharding import Mesh
from jax.sharding import PartitionSpec as P

off_weight = 0.0051
eps = 1e-05
DP = ("x", "y", "c")


def shift(v, axis, n, step):
    return lax.ppermute(v, axis, [(i, (i + step) % n) for i in range(n)])


def ring_gather(v, axis):
    n = lax.axis_size(axis)
    if n == 1:
        return v[None]
    right = n // 2
    left = n - 1 - right
    got = {0: v}
    cur = v
    for s in range(1, right + 1):
        cur = shift(cur, axis, n, 1)
        got[n - s] = cur
    cur = v
    for s in range(1, left + 1):
        cur = shift(cur, axis, n, -1)
        got[s] = cur
    return jnp.stack([got[t] for t in range(n)])


def dp_ring_gather(v):
    return ring_gather(ring_gather(ring_gather(v, "x"), "y"), "c")


def combine(mean, m2, count, axis, k):
    n = lax.axis_size(axis)
    pairs = [(i, i ^ k) for i in range(n)]
    other_mean = lax.ppermute(mean, axis, pairs)
    other_m2 = lax.ppermute(m2, axis, pairs)
    delta = other_mean - mean
    new_mean = (mean + other_mean) * 0.5
    new_m2 = (m2 + other_m2) + delta * delta * (count * 0.5)
    return new_mean, new_m2, count * 2


def dp_stats(feats):
    local = feats.shape[1]
    mean = jnp.sum(feats, axis=1, keepdims=True) / local
    dev = feats - mean
    m2 = jnp.sum(dev * dev, axis=1, keepdims=True)
    count = float(local)
    for axis in ("c", "y", "x"):
        k = 1
        while k < lax.axis_size(axis):
            mean, m2, count = combine(mean, m2, count, axis, k)
            k *= 2
    return mean, m2 / count


def relative_order(v, axes):
    for dim, axis in enumerate(axes, start=1):
        v = jnp.roll(v, -lax.axis_index(axis), axis=dim)
    return v


def shards(hidden, proj_weight):
    mp_index = lax.axis_index("mp")
    dp_index = lax.axis_index(DP)
    dp_count = lax.axis_size(DP)
    nx, ny, nc = lax.axis_size("x"), lax.axis_size("y"), lax.axis_size("c")
    ix, iy, ic = lax.axis_index("x"), lax.axis_index("y"), lax.axis_index("c")
    rows = proj_weight.shape[1]
    local = hidden.shape[1]
    total = local * dp_count
    feats = jnp.einsum("vbh,hc->vbc", hidden, proj_weight, preferred_element_type=jnp.float32)
    mean, var = dp_stats(feats)
    centered = feats - mean
    normed = (centered / jnp.sqrt(var + eps)).astype(jnp.bfloat16)
    inv_std = 1.0 / jnp.sqrt(var + eps)
    first = normed[0]
    second = normed[1]
    n_mp = lax.axis_size("mp")
    stacked = lax.all_gather(second, "mp", axis=0)
    second_full = jnp.transpose(stacked, (1, 0, 2)).reshape(local, n_mp * rows)
    width = second_full.shape[1] // dp_count
    columns = lax.all_to_all(second_full, DP, split_axis=1, concat_axis=0, tiled=True)
    columns = relative_order(columns.reshape(1, nx, ny, nc, local, width), ("x", "y", "c"))
    columns = jnp.transpose(columns[0], (2, 1, 0, 3, 4)).reshape(total, width)
    first_all = dp_ring_gather(first).reshape(total, rows)
    corr = (
        jnp.einsum("bi,bj->ij", first_all, columns, preferred_element_type=jnp.float32)
        / total
    )
    row_ids = mp_index * rows + lax.iota(jnp.int32, rows)[:, None]
    col_ids = dp_index * width + lax.iota(jnp.int32, width)[None, :]
    grad_block = jnp.where(row_ids == col_ids, 2.0 * (corr - 1.0), 2.0 * off_weight * corr).astype(
        jnp.bfloat16
    )
    grad_t = dp_ring_gather(grad_block.T).reshape(dp_count * width, rows)
    t = lax.iota(jnp.int32, width)
    cc = (lax.iota(jnp.int32, nc) + ic) % nc
    yy = (lax.iota(jnp.int32, ny) + iy) % ny
    xx = (lax.iota(jnp.int32, nx) + ix) % nx
    perm_cols = (
        ((xx[None, None, :, None] * ny + yy[None, :, None, None]) * nc + cc[:, None, None, None]) * width
        + t[None, None, None, :]
    ).reshape(-1)
    grad_wide = grad_t.astype(jnp.float32)
    row_flat = mp_index * rows + lax.iota(jnp.int32, rows)
    diag_val = jnp.sum(jnp.where(perm_cols[:, None] == row_flat[None, :], grad_wide, 0.0), axis=0)
    scale_sum = (jnp.sum(grad_wide * grad_wide, axis=0) - diag_val * diag_val) / (
        2.0 * off_weight
    ) + diag_val * (1.0 + diag_val / 2.0)
    second_perm = relative_order(second_full.reshape(local, nx, ny, nc, width), ("x", "y", "c"))
    second_perm = jnp.transpose(second_perm, (0, 3, 2, 1, 4)).reshape(local, dp_count * width)
    back = jnp.dot(second_perm, grad_t, preferred_element_type=jnp.float32)
    result = (back - first.astype(jnp.float32) * scale_sum[None, :]) * inv_std[0]
    return result.astype(jnp.bfloat16)


def solution(mesh):
    x, y, c = (4, 8, 2)
    sub = Mesh(mesh.devices.reshape(x, y, c, mesh.devices.shape[1]), DP + ("mp",))
    return jax.shard_map(
        shards,
        mesh=sub,
        in_specs=(P(None, DP, None), P(None, "mp")),
        out_specs=P(DP, "mp"),
        check_vma=False,
    )
```

```python
import jax
import jax.numpy as jnp
from jax import lax
from jax.sharding import Mesh
from jax.sharding import PartitionSpec as P

off_weight = 0.0051
eps = 1e-05
DP = ("x", "y", "c")


def shift(v, axis, n, step):
    return lax.ppermute(v, axis, [(i, (i + step) % n) for i in range(n)])


def ring_gather(v, axis):
    n = lax.axis_size(axis)
    if n == 1:
        return v[None]
    right = n // 2
    left = n - 1 - right
    got = {0: v}
    cur = v
    for s in range(1, right + 1):
        cur = shift(cur, axis, n, 1)
        got[n - s] = cur
    cur = v
    for s in range(1, left + 1):
        cur = shift(cur, axis, n, -1)
        got[s] = cur
    return jnp.stack([got[t] for t in range(n)])


def dp_ring_gather(v):
    return ring_gather(ring_gather(ring_gather(v, "x"), "y"), "c")


def combine(mean, m2, count, axis, k):
    n = lax.axis_size(axis)
    pairs = [(i, i ^ k) for i in range(n)]
    other = lax.ppermute(jnp.stack([mean, m2]), axis, pairs)
    other_mean, other_m2 = other[0], other[1]
    delta = other_mean - mean
    new_mean = (mean + other_mean) * 0.5
    new_m2 = (m2 + other_m2) + delta * delta * (count * 0.5)
    return new_mean, new_m2, count * 2


def dp_stats(feats):
    local = feats.shape[1]
    mean = jnp.sum(feats, axis=1, keepdims=True) / local
    dev = feats - mean
    m2 = jnp.sum(dev * dev, axis=1, keepdims=True)
    count = float(local)
    for axis in ("c", "y", "x"):
        k = 1
        while k < lax.axis_size(axis):
            mean, m2, count = combine(mean, m2, count, axis, k)
            k *= 2
    return mean, m2 / count


def relative_order(v, axes):
    for dim, axis in enumerate(axes, start=1):
        v = jnp.roll(v, -lax.axis_index(axis), axis=dim)
    return v


def shards(hidden, proj_weight):
    mp_index = lax.axis_index("mp")
    dp_index = lax.axis_index(DP)
    dp_count = lax.axis_size(DP)
    nx, ny, nc = lax.axis_size("x"), lax.axis_size("y"), lax.axis_size("c")
    ix, iy, ic = lax.axis_index("x"), lax.axis_index("y"), lax.axis_index("c")
    rows = proj_weight.shape[1]
    local = hidden.shape[1]
    total = local * dp_count
    feats = jnp.einsum("vbh,hc->vbc", hidden, proj_weight, preferred_element_type=jnp.float32)
    mean, var = dp_stats(feats)
    centered = feats - mean
    normed = (centered / jnp.sqrt(var + eps)).astype(jnp.bfloat16)
    inv_std = 1.0 / jnp.sqrt(var + eps)
    first = normed[0]
    second = normed[1]
    n_mp = lax.axis_size("mp")
    stacked = lax.all_gather(second, "mp", axis=0)
    second_full = jnp.transpose(stacked, (1, 0, 2)).reshape(local, n_mp * rows)
    width = second_full.shape[1] // dp_count
    columns = lax.all_to_all(second_full, DP, split_axis=1, concat_axis=0, tiled=True)
    first_all = lax.all_gather(first, DP, axis=0, tiled=True)
    corr = (
        jnp.einsum("bi,bj->ij", first_all, columns, preferred_element_type=jnp.float32)
        / total
    )
    row_ids = mp_index * rows + lax.iota(jnp.int32, rows)[:, None]
    col_ids = dp_index * width + lax.iota(jnp.int32, width)[None, :]
    grad_block = jnp.where(row_ids == col_ids, 2.0 * (corr - 1.0), 2.0 * off_weight * corr).astype(
        jnp.bfloat16
    )
    grad_t = dp_ring_gather(grad_block.T).reshape(dp_count * width, rows)
    t = lax.iota(jnp.int32, width)
    cc = (lax.iota(jnp.int32, nc) + ic) % nc
    yy = (lax.iota(jnp.int32, ny) + iy) % ny
    xx = (lax.iota(jnp.int32, nx) + ix) % nx
    perm_cols = (
        ((xx[None, None, :, None] * ny + yy[None, :, None, None]) * nc + cc[:, None, None, None]) * width
        + t[None, None, None, :]
    ).reshape(-1)
    grad_wide = grad_t.astype(jnp.float32)
    row_flat = mp_index * rows + lax.iota(jnp.int32, rows)
    diag_val = jnp.sum(jnp.where(perm_cols[:, None] == row_flat[None, :], grad_wide, 0.0), axis=0)
    scale_sum = (jnp.sum(grad_wide * grad_wide, axis=0) - diag_val * diag_val) / (
        2.0 * off_weight
    ) + diag_val * (1.0 + diag_val / 2.0)
    second_perm = relative_order(second_full.reshape(local, nx, ny, nc, width), ("x", "y", "c"))
    second_perm = jnp.transpose(second_perm, (0, 3, 2, 1, 4)).reshape(local, dp_count * width)
    back = jnp.dot(second_perm, grad_t, preferred_element_type=jnp.float32)
    result = (back - first.astype(jnp.float32) * scale_sum[None, :]) * inv_std[0]
    return result.astype(jnp.bfloat16)


def solution(mesh):
    x, y, c = (4, 8, 2)
    sub = Mesh(mesh.devices.reshape(x, y, c, mesh.devices.shape[1]), DP + ("mp",))
    return jax.shard_map(
        shards,
        mesh=sub,
        in_specs=(P(None, DP, None), P(None, "mp")),
        out_specs=P(DP, "mp"),
        check_vma=False,
    )
```

```python
import jax
import jax.numpy as jnp
from jax import lax
from jax.sharding import Mesh
from jax.sharding import PartitionSpec as P

off_weight = 0.0051
eps = 1e-05
DP = ("x", "y", "c")


def shift(v, axis, n, step):
    return lax.ppermute(v, axis, [(i, (i + step) % n) for i in range(n)])


def ring_gather(v, axis):
    n = lax.axis_size(axis)
    if n == 1:
        return v[None]
    right = n // 2
    left = n - 1 - right
    got = {0: v}
    cur = v
    for s in range(1, right + 1):
        cur = shift(cur, axis, n, 1)
        got[n - s] = cur
    cur = v
    for s in range(1, left + 1):
        cur = shift(cur, axis, n, -1)
        got[s] = cur
    return jnp.stack([got[t] for t in range(n)])


def dp_ring_gather(v):
    return ring_gather(ring_gather(ring_gather(v, "x"), "y"), "c")


def combine(mean, m2, count, axis, k):
    n = lax.axis_size(axis)
    pairs = [(i, i ^ k) for i in range(n)]
    other = lax.ppermute(jnp.stack([mean, m2]), axis, pairs)
    other_mean, other_m2 = other[0], other[1]
    delta = other_mean - mean
    new_mean = (mean + other_mean) * 0.5
    new_m2 = (m2 + other_m2) + delta * delta * (count * 0.5)
    return new_mean, new_m2, count * 2


def dp_stats(feats):
    local = feats.shape[1]
    mean = jnp.sum(feats, axis=1, keepdims=True) / local
    dev = feats - mean
    m2 = jnp.sum(dev * dev, axis=1, keepdims=True)
    count = float(local)
    for axis in ("c", "y", "x"):
        k = 1
        while k < lax.axis_size(axis):
            mean, m2, count = combine(mean, m2, count, axis, k)
            k *= 2
    return mean, m2 / count


def relative_order(v, axes):
    for dim, axis in enumerate(axes, start=1):
        v = jnp.roll(v, -lax.axis_index(axis), axis=dim)
    return v


def shards(hidden, proj_weight):
    mp_index = lax.axis_index("mp")
    dp_index = lax.axis_index(DP)
    dp_count = lax.axis_size(DP)
    nx, ny, nc = lax.axis_size("x"), lax.axis_size("y"), lax.axis_size("c")
    ix, iy, ic = lax.axis_index("x"), lax.axis_index("y"), lax.axis_index("c")
    rows = proj_weight.shape[1]
    local = hidden.shape[1]
    total = local * dp_count
    feats = jnp.einsum("vbh,hc->vbc", hidden, proj_weight, preferred_element_type=jnp.float32)
    mean, var = dp_stats(feats)
    centered = feats - mean
    normed = (centered / jnp.sqrt(var + eps)).astype(jnp.bfloat16)
    inv_std = 1.0 / jnp.sqrt(var + eps)
    first = normed[0]
    second = normed[1]
    n_mp = lax.axis_size("mp")
    stacked = lax.all_gather(second, "mp", axis=0)
    second_full = jnp.transpose(stacked, (1, 0, 2)).reshape(local, n_mp * rows)
    width = second_full.shape[1] // dp_count
    columns = lax.all_to_all(second_full, DP, split_axis=1, concat_axis=0, tiled=True)
    half = rows // 2
    first_all = jnp.concatenate([lax.all_gather(first[:, :half], DP, axis=0, tiled=True), lax.all_gather(first[:, half:], DP, axis=0, tiled=True)], axis=1)
    corr = (
        jnp.einsum("bi,bj->ij", first_all, columns, preferred_element_type=jnp.float32)
        / total
    )
    row_ids = mp_index * rows + lax.iota(jnp.int32, rows)[:, None]
    col_ids = dp_index * width + lax.iota(jnp.int32, width)[None, :]
    grad_block = jnp.where(row_ids == col_ids, 2.0 * (corr - 1.0), 2.0 * off_weight * corr).astype(
        jnp.bfloat16
    )
    grad_t = dp_ring_gather(grad_block.T).reshape(dp_count * width, rows)
    t = lax.iota(jnp.int32, width)
    cc = (lax.iota(jnp.int32, nc) + ic) % nc
    yy = (lax.iota(jnp.int32, ny) + iy) % ny
    xx = (lax.iota(jnp.int32, nx) + ix) % nx
    perm_cols = (
        ((xx[None, None, :, None] * ny + yy[None, :, None, None]) * nc + cc[:, None, None, None]) * width
        + t[None, None, None, :]
    ).reshape(-1)
    grad_wide = grad_t.astype(jnp.float32)
    row_flat = mp_index * rows + lax.iota(jnp.int32, rows)
    diag_val = jnp.sum(jnp.where(perm_cols[:, None] == row_flat[None, :], grad_wide, 0.0), axis=0)
    scale_sum = (jnp.sum(grad_wide * grad_wide, axis=0) - diag_val * diag_val) / (
        2.0 * off_weight
    ) + diag_val * (1.0 + diag_val / 2.0)
    second_perm = relative_order(second_full.reshape(local, nx, ny, nc, width), ("x", "y", "c"))
    second_perm = jnp.transpose(second_perm, (0, 3, 2, 1, 4)).reshape(local, dp_count * width)
    back = jnp.dot(second_perm, grad_t, preferred_element_type=jnp.float32)
    result = (back - first.astype(jnp.float32) * scale_sum[None, :]) * inv_std[0]
    return result.astype(jnp.bfloat16)


def solution(mesh):
    x, y, c = (4, 8, 2)
    sub = Mesh(mesh.devices.reshape(x, y, c, mesh.devices.shape[1]), DP + ("mp",))
    return jax.shard_map(
        shards,
        mesh=sub,
        in_specs=(P(None, DP, None), P(None, "mp")),
        out_specs=P(DP, "mp"),
        check_vma=False,
    )
```

```python
import jax
import jax.numpy as jnp
from jax import lax
from jax.sharding import Mesh
from jax.sharding import PartitionSpec as P

off_weight = 0.0051
eps = 1e-05
DP = ("x", "y", "c")


def shift(v, axis, n, step):
    return lax.ppermute(v, axis, [(i, (i + step) % n) for i in range(n)])


def ring_gather(v, axis):
    n = lax.axis_size(axis)
    if n == 1:
        return v[None]
    right = n // 2
    left = n - 1 - right
    got = {0: v}
    cur = v
    for s in range(1, right + 1):
        cur = shift(cur, axis, n, 1)
        got[n - s] = cur
    cur = v
    for s in range(1, left + 1):
        cur = shift(cur, axis, n, -1)
        got[s] = cur
    return jnp.stack([got[t] for t in range(n)])


def dp_ring_gather(v):
    return ring_gather(ring_gather(ring_gather(v, "x"), "y"), "c")


def combine(mean, m2, count, axis, k):
    n = lax.axis_size(axis)
    pairs = [(i, i ^ k) for i in range(n)]
    other = lax.ppermute(jnp.stack([mean, m2]), axis, pairs)
    other_mean, other_m2 = other[0], other[1]
    delta = other_mean - mean
    new_mean = (mean + other_mean) * 0.5
    new_m2 = (m2 + other_m2) + delta * delta * (count * 0.5)
    return new_mean, new_m2, count * 2


def dp_stats(feats):
    local = feats.shape[1]
    mean = jnp.sum(feats, axis=1, keepdims=True) / local
    dev = feats - mean
    m2 = jnp.sum(dev * dev, axis=1, keepdims=True)
    count = float(local)
    for axis in ("c", "y", "x"):
        k = 1
        while k < lax.axis_size(axis):
            mean, m2, count = combine(mean, m2, count, axis, k)
            k *= 2
    return mean, m2 / count


def relative_order(v, axes):
    for dim, axis in enumerate(axes, start=1):
        v = jnp.roll(v, -lax.axis_index(axis), axis=dim)
    return v


def shards(hidden, proj_weight):
    mp_index = lax.axis_index("mp")
    dp_index = lax.axis_index(DP)
    dp_count = lax.axis_size(DP)
    nx, ny, nc = lax.axis_size("x"), lax.axis_size("y"), lax.axis_size("c")
    ix, iy, ic = lax.axis_index("x"), lax.axis_index("y"), lax.axis_index("c")
    rows = proj_weight.shape[1]
    local = hidden.shape[1]
    total = local * dp_count
    feats = jnp.einsum("vbh,hc->vbc", hidden, proj_weight, preferred_element_type=jnp.float32)
    mean, var = dp_stats(feats)
    centered = feats - mean
    normed = (centered / jnp.sqrt(var + eps)).astype(jnp.bfloat16)
    inv_std = 1.0 / jnp.sqrt(var + eps)
    first = normed[0]
    second = normed[1]
    n_mp = lax.axis_size("mp")
    stacked = lax.all_gather(second, "mp", axis=0)
    second_full = jnp.transpose(stacked, (1, 0, 2)).reshape(local, n_mp * rows)
    width = second_full.shape[1] // dp_count
    columns = lax.all_to_all(second_full, DP, split_axis=1, concat_axis=0, tiled=True)
    second_perm = relative_order(second_full.reshape(local, nx, ny, nc, width), ("x", "y", "c"))
    second_perm = jnp.transpose(second_perm, (0, 3, 2, 1, 4)).reshape(local, dp_count * width)
    columns, second_perm = lax.optimization_barrier((columns, second_perm))
    first_all = lax.all_gather(first, DP, axis=0, tiled=True)
    corr = (
        jnp.einsum("bi,bj->ij", first_all, columns, preferred_element_type=jnp.float32)
        / total
    )
    row_ids = mp_index * rows + lax.iota(jnp.int32, rows)[:, None]
    col_ids = dp_index * width + lax.iota(jnp.int32, width)[None, :]
    grad_block = jnp.where(row_ids == col_ids, 2.0 * (corr - 1.0), 2.0 * off_weight * corr).astype(
        jnp.bfloat16
    )
    grad_t = dp_ring_gather(grad_block.T).reshape(dp_count * width, rows)
    t = lax.iota(jnp.int32, width)
    cc = (lax.iota(jnp.int32, nc) + ic) % nc
    yy = (lax.iota(jnp.int32, ny) + iy) % ny
    xx = (lax.iota(jnp.int32, nx) + ix) % nx
    perm_cols = (
        ((xx[None, None, :, None] * ny + yy[None, :, None, None]) * nc + cc[:, None, None, None]) * width
        + t[None, None, None, :]
    ).reshape(-1)
    grad_wide = grad_t.astype(jnp.float32)
    row_flat = mp_index * rows + lax.iota(jnp.int32, rows)
    diag_val = jnp.sum(jnp.where(perm_cols[:, None] == row_flat[None, :], grad_wide, 0.0), axis=0)
    scale_sum = (jnp.sum(grad_wide * grad_wide, axis=0) - diag_val * diag_val) / (
        2.0 * off_weight
    ) + diag_val * (1.0 + diag_val / 2.0)
    back = jnp.dot(second_perm, grad_t, preferred_element_type=jnp.float32)
    result = (back - first.astype(jnp.float32) * scale_sum[None, :]) * inv_std[0]
    return result.astype(jnp.bfloat16)


def solution(mesh):
    x, y, c = (4, 8, 2)
    sub = Mesh(mesh.devices.reshape(x, y, c, mesh.devices.shape[1]), DP + ("mp",))
    return jax.shard_map(
        shards,
        mesh=sub,
        in_specs=(P(None, DP, None), P(None, "mp")),
        out_specs=P(DP, "mp"),
        check_vma=False,
    )
```

```python
import jax
import jax.numpy as jnp
from jax import lax
from jax.sharding import Mesh
from jax.sharding import PartitionSpec as P

off_weight = 0.0051
eps = 1e-05
DP = ("x", "y", "c")


def shift(v, axis, n, step):
    return lax.ppermute(v, axis, [(i, (i + step) % n) for i in range(n)])


def ring_gather(v, axis):
    n = lax.axis_size(axis)
    if n == 1:
        return v[None]
    right = n // 2
    left = n - 1 - right
    got = {0: v}
    cur = v
    for s in range(1, right + 1):
        cur = shift(cur, axis, n, 1)
        got[n - s] = cur
    cur = v
    for s in range(1, left + 1):
        cur = shift(cur, axis, n, -1)
        got[s] = cur
    return jnp.stack([got[t] for t in range(n)])


def dp_ring_gather(v):
    return ring_gather(ring_gather(ring_gather(v, "x"), "y"), "c")


def combine(mean, m2, count, axis, k):
    n = lax.axis_size(axis)
    pairs = [(i, i ^ k) for i in range(n)]
    other = lax.ppermute(jnp.stack([mean, m2]), axis, pairs)
    other_mean, other_m2 = other[0], other[1]
    delta = other_mean - mean
    new_mean = (mean + other_mean) * 0.5
    new_m2 = (m2 + other_m2) + delta * delta * (count * 0.5)
    return new_mean, new_m2, count * 2


def dp_stats(feats):
    local = feats.shape[1]
    mean = jnp.sum(feats, axis=1, keepdims=True) / local
    dev = feats - mean
    m2 = jnp.sum(dev * dev, axis=1, keepdims=True)
    count = float(local)
    for axis in ("c", "y", "x"):
        k = 1
        while k < lax.axis_size(axis):
            mean, m2, count = combine(mean, m2, count, axis, k)
            k *= 2
    return mean, m2 / count


def relative_order(v, axes):
    for dim, axis in enumerate(axes, start=1):
        v = jnp.roll(v, -lax.axis_index(axis), axis=dim)
    return v


def shards(hidden, proj_weight):
    mp_index = lax.axis_index("mp")
    dp_index = lax.axis_index(DP)
    dp_count = lax.axis_size(DP)
    nx, ny, nc = lax.axis_size("x"), lax.axis_size("y"), lax.axis_size("c")
    ix, iy, ic = lax.axis_index("x"), lax.axis_index("y"), lax.axis_index("c")
    rows = proj_weight.shape[1]
    local = hidden.shape[1]
    total = local * dp_count
    feats = jnp.einsum("vbh,hc->vbc", hidden, proj_weight, preferred_element_type=jnp.float32)
    feats0_all = lax.all_gather(feats[0], DP, axis=0, tiled=True)
    mean0 = jnp.sum(feats0_all, axis=0, keepdims=True) / total
    centered0 = feats0_all - mean0
    var0 = jnp.sum(centered0 * centered0, axis=0, keepdims=True) / total
    first_all = (centered0 / jnp.sqrt(var0 + eps)).astype(jnp.bfloat16)
    first = ((feats[0] - mean0) / jnp.sqrt(var0 + eps)).astype(jnp.bfloat16)
    inv_std0 = 1.0 / jnp.sqrt(var0 + eps)
    mean1, var1 = dp_stats(feats[1:])
    second = ((feats[1] - mean1[0]) / jnp.sqrt(var1[0] + eps)).astype(jnp.bfloat16)
    n_mp = lax.axis_size("mp")
    stacked = lax.all_gather(second, "mp", axis=0)
    second_full = jnp.transpose(stacked, (1, 0, 2)).reshape(local, n_mp * rows)
    width = second_full.shape[1] // dp_count
    columns = lax.all_to_all(second_full, DP, split_axis=1, concat_axis=0, tiled=True)
    second_perm = relative_order(second_full.reshape(local, nx, ny, nc, width), ("x", "y", "c"))
    second_perm = jnp.transpose(second_perm, (0, 3, 2, 1, 4)).reshape(local, dp_count * width)
    columns, second_perm = lax.optimization_barrier((columns, second_perm))
    corr = (
        jnp.einsum("bi,bj->ij", first_all, columns, preferred_element_type=jnp.float32)
        / total
    )
    row_ids = mp_index * rows + lax.iota(jnp.int32, rows)[:, None]
    col_ids = dp_index * width + lax.iota(jnp.int32, width)[None, :]
    grad_block = jnp.where(row_ids == col_ids, 2.0 * (corr - 1.0), 2.0 * off_weight * corr).astype(
        jnp.bfloat16
    )
    grad_t = dp_ring_gather(grad_block.T).reshape(dp_count * width, rows)
    t = lax.iota(jnp.int32, width)
    cc = (lax.iota(jnp.int32, nc) + ic) % nc
    yy = (lax.iota(jnp.int32, ny) + iy) % ny
    xx = (lax.iota(jnp.int32, nx) + ix) % nx
    perm_cols = (
        ((xx[None, None, :, None] * ny + yy[None, :, None, None]) * nc + cc[:, None, None, None]) * width
        + t[None, None, None, :]
    ).reshape(-1)
    grad_wide = grad_t.astype(jnp.float32)
    row_flat = mp_index * rows + lax.iota(jnp.int32, rows)
    diag_val = jnp.sum(jnp.where(perm_cols[:, None] == row_flat[None, :], grad_wide, 0.0), axis=0)
    scale_sum = (jnp.sum(grad_wide * grad_wide, axis=0) - diag_val * diag_val) / (
        2.0 * off_weight
    ) + diag_val * (1.0 + diag_val / 2.0)
    back = jnp.dot(second_perm, grad_t, preferred_element_type=jnp.float32)
    result = (back - first.astype(jnp.float32) * scale_sum[None, :]) * inv_std0
    return result.astype(jnp.bfloat16)


def solution(mesh):
    x, y, c = (4, 8, 2)
    sub = Mesh(mesh.devices.reshape(x, y, c, mesh.devices.shape[1]), DP + ("mp",))
    return jax.shard_map(
        shards,
        mesh=sub,
        in_specs=(P(None, DP, None), P(None, "mp")),
        out_specs=P(DP, "mp"),
        check_vma=False,
    )
```

```python
import jax
import jax.numpy as jnp
from jax import lax
from jax.sharding import Mesh
from jax.sharding import PartitionSpec as P

off_weight = 0.0051
eps = 1e-05
DP = ("x", "y", "c")


def shift(v, axis, n, step):
    return lax.ppermute(v, axis, [(i, (i + step) % n) for i in range(n)])


def ring_gather(v, axis):
    n = lax.axis_size(axis)
    if n == 1:
        return v[None]
    right = n // 2
    left = n - 1 - right
    got = {0: v}
    cur = v
    for s in range(1, right + 1):
        cur = shift(cur, axis, n, 1)
        got[n - s] = cur
    cur = v
    for s in range(1, left + 1):
        cur = shift(cur, axis, n, -1)
        got[s] = cur
    return jnp.stack([got[t] for t in range(n)])


def ring_gather_abs(v, axis):
    return jnp.roll(ring_gather(v, axis), lax.axis_index(axis), axis=0)


def dp_ring_gather(v):
    g = ring_gather_abs(ring_gather_abs(ring_gather_abs(v, "x"), "y"), "c")
    return jnp.transpose(g, (2, 1, 0) + tuple(range(3, g.ndim)))


def combine(mean, m2, count, axis, k):
    n = lax.axis_size(axis)
    pairs = [(i, i ^ k) for i in range(n)]
    other = lax.ppermute(jnp.stack([mean, m2]), axis, pairs)
    other_mean, other_m2 = other[0], other[1]
    delta = other_mean - mean
    new_mean = (mean + other_mean) * 0.5
    new_m2 = (m2 + other_m2) + delta * delta * (count * 0.5)
    return new_mean, new_m2, count * 2


def dp_stats(feats):
    local = feats.shape[1]
    mean = jnp.sum(feats, axis=1, keepdims=True) / local
    dev = feats - mean
    m2 = jnp.sum(dev * dev, axis=1, keepdims=True)
    count = float(local)
    for axis in ("c", "y", "x"):
        k = 1
        while k < lax.axis_size(axis):
            mean, m2, count = combine(mean, m2, count, axis, k)
            k *= 2
    return mean, m2 / count


def shards(hidden, proj_weight):
    mp_index = lax.axis_index("mp")
    dp_index = lax.axis_index(DP)
    dp_count = lax.axis_size(DP)
    rows = proj_weight.shape[1]
    local = hidden.shape[1]
    total = local * dp_count
    feats = jnp.einsum("vbh,hc->vbc", hidden, proj_weight, preferred_element_type=jnp.float32)
    feats0_all = lax.all_gather(feats[0], DP, axis=0, tiled=True)
    mean0 = jnp.sum(feats0_all, axis=0, keepdims=True) / total
    centered0 = feats0_all - mean0
    var0 = jnp.sum(centered0 * centered0, axis=0, keepdims=True) / total
    first_all = (centered0 / jnp.sqrt(var0 + eps)).astype(jnp.bfloat16)
    first = ((feats[0] - mean0) / jnp.sqrt(var0 + eps)).astype(jnp.bfloat16)
    inv_std0 = 1.0 / jnp.sqrt(var0 + eps)
    mean1, var1 = dp_stats(feats[1:])
    second = ((feats[1] - mean1[0]) / jnp.sqrt(var1[0] + eps)).astype(jnp.bfloat16)
    n_mp = lax.axis_size("mp")
    stacked = lax.all_gather(second, "mp", axis=0)
    second_full = jnp.transpose(stacked, (1, 0, 2)).reshape(local, n_mp * rows)
    width = second_full.shape[1] // dp_count
    columns = lax.all_to_all(second_full, DP, split_axis=1, concat_axis=0, tiled=True)
    corr = (
        jnp.einsum("bi,bj->ij", first_all, columns, preferred_element_type=jnp.float32)
        / total
    )
    row_ids = mp_index * rows + lax.iota(jnp.int32, rows)[:, None]
    col_ids = dp_index * width + lax.iota(jnp.int32, width)[None, :]
    grad_block = jnp.where(row_ids == col_ids, 2.0 * (corr - 1.0), 2.0 * off_weight * corr).astype(
        jnp.bfloat16
    )
    grad_t = dp_ring_gather(grad_block.T).reshape(dp_count * width, rows)
    grad_wide = grad_t.astype(jnp.float32)
    all_cols = lax.iota(jnp.int32, dp_count * width)
    row_flat = mp_index * rows + lax.iota(jnp.int32, rows)
    diag_val = jnp.sum(jnp.where(all_cols[:, None] == row_flat[None, :], grad_wide, 0.0), axis=0)
    scale_sum = (jnp.sum(grad_wide * grad_wide, axis=0) - diag_val * diag_val) / (
        2.0 * off_weight
    ) + diag_val * (1.0 + diag_val / 2.0)
    back = jnp.dot(second_full, grad_t, preferred_element_type=jnp.float32)
    result = (back - first.astype(jnp.float32) * scale_sum[None, :]) * inv_std0
    return result.astype(jnp.bfloat16)


def solution(mesh):
    x, y, c = (4, 8, 2)
    sub = Mesh(mesh.devices.reshape(x, y, c, mesh.devices.shape[1]), DP + ("mp",))
    return jax.shard_map(
        shards,
        mesh=sub,
        in_specs=(P(None, DP, None), P(None, "mp")),
        out_specs=P(DP, "mp"),
        check_vma=False,
    )
```

```python
import jax
import jax.numpy as jnp
from jax import lax
from jax.sharding import Mesh
from jax.sharding import PartitionSpec as P

off_weight = 0.0051
eps = 1e-05
DP = ("x", "y", "c")


def shift(v, axis, n, step):
    return lax.ppermute(v, axis, [(i, (i + step) % n) for i in range(n)])


def ring_gather(v, axis):
    n = lax.axis_size(axis)
    if n == 1:
        return v[None]
    right = n // 2
    left = n - 1 - right
    got = {0: v}
    cur = v
    for s in range(1, right + 1):
        cur = shift(cur, axis, n, 1)
        got[n - s] = cur
    cur = v
    for s in range(1, left + 1):
        cur = shift(cur, axis, n, -1)
        got[s] = cur
    return jnp.stack([got[t] for t in range(n)])


def dp_ring_gather(v):
    return ring_gather(ring_gather(ring_gather(v, "x"), "y"), "c")


def combine(mean, m2, count, axis, k):
    n = lax.axis_size(axis)
    pairs = [(i, i ^ k) for i in range(n)]
    other = lax.ppermute(jnp.stack([mean, m2]), axis, pairs)
    other_mean, other_m2 = other[0], other[1]
    delta = other_mean - mean
    new_mean = (mean + other_mean) * 0.5
    new_m2 = (m2 + other_m2) + delta * delta * (count * 0.5)
    return new_mean, new_m2, count * 2


def dp_stats(feats):
    local = feats.shape[1]
    mean = jnp.sum(feats, axis=1, keepdims=True) / local
    dev = feats - mean
    m2 = jnp.sum(dev * dev, axis=1, keepdims=True)
    count = float(local)
    for axis in ("c", "y", "x"):
        k = 1
        while k < lax.axis_size(axis):
            mean, m2, count = combine(mean, m2, count, axis, k)
            k *= 2
    return mean, m2 / count


def relative_order(v, axes):
    for dim, axis in enumerate(axes, start=1):
        v = jnp.roll(v, -lax.axis_index(axis), axis=dim)
    return v


def shards(hidden, proj_weight):
    mp_index = lax.axis_index("mp")
    dp_index = lax.axis_index(DP)
    dp_count = lax.axis_size(DP)
    nx, ny, nc = lax.axis_size("x"), lax.axis_size("y"), lax.axis_size("c")
    ix, iy, ic = lax.axis_index("x"), lax.axis_index("y"), lax.axis_index("c")
    rows = proj_weight.shape[1]
    local = hidden.shape[1]
    total = local * dp_count
    feats = jnp.einsum("vbh,hc->vbc", hidden, proj_weight, preferred_element_type=jnp.float32)
    feats0_all = lax.all_gather(feats[0], DP, axis=0, tiled=True)
    mean0 = jnp.sum(feats0_all, axis=0, keepdims=True) / total
    centered0 = feats0_all - mean0
    var0 = jnp.sum(centered0 * centered0, axis=0, keepdims=True) / total
    first_all = (centered0 / jnp.sqrt(var0 + eps)).astype(jnp.bfloat16)
    first = ((feats[0] - mean0) / jnp.sqrt(var0 + eps)).astype(jnp.bfloat16)
    inv_std0 = 1.0 / jnp.sqrt(var0 + eps)
    n_mp = lax.axis_size("mp")
    stacked = lax.all_gather(feats[1], "mp", axis=0)
    raw_full = jnp.transpose(stacked, (1, 0, 2)).reshape(local, n_mp * rows)
    width = raw_full.shape[1] // dp_count
    raw_cols = lax.all_to_all(raw_full, DP, split_axis=1, concat_axis=0, tiled=True)
    mean_c = jnp.sum(raw_cols, axis=0, keepdims=True) / total
    centered_c = raw_cols - mean_c
    var_c = jnp.sum(centered_c * centered_c, axis=0, keepdims=True) / total
    columns = (centered_c / jnp.sqrt(var_c + eps)).astype(jnp.bfloat16)
    mean1, var1 = dp_stats(raw_full[None])
    second_full = ((raw_full - mean1[0]) / jnp.sqrt(var1[0] + eps)).astype(jnp.bfloat16)
    second_perm = relative_order(second_full.reshape(local, nx, ny, nc, width), ("x", "y", "c"))
    second_perm = jnp.transpose(second_perm, (0, 3, 2, 1, 4)).reshape(local, dp_count * width)
    corr = (
        jnp.einsum("bi,bj->ij", first_all, columns, preferred_element_type=jnp.float32)
        / total
    )
    row_ids = mp_index * rows + lax.iota(jnp.int32, rows)[:, None]
    col_ids = dp_index * width + lax.iota(jnp.int32, width)[None, :]
    grad_block = jnp.where(row_ids == col_ids, 2.0 * (corr - 1.0), 2.0 * off_weight * corr).astype(
        jnp.bfloat16
    )
    grad_block, second_perm = lax.optimization_barrier((grad_block, second_perm))
    grad_t = dp_ring_gather(grad_block.T).reshape(dp_count * width, rows)
    t = lax.iota(jnp.int32, width)
    cc = (lax.iota(jnp.int32, nc) + ic) % nc
    yy = (lax.iota(jnp.int32, ny) + iy) % ny
    xx = (lax.iota(jnp.int32, nx) + ix) % nx
    perm_cols = (
        ((xx[None, None, :, None] * ny + yy[None, :, None, None]) * nc + cc[:, None, None, None]) * width
        + t[None, None, None, :]
    ).reshape(-1)
    grad_wide = grad_t.astype(jnp.float32)
    row_flat = mp_index * rows + lax.iota(jnp.int32, rows)
    diag_val = jnp.sum(jnp.where(perm_cols[:, None] == row_flat[None, :], grad_wide, 0.0), axis=0)
    scale_sum = (jnp.sum(grad_wide * grad_wide, axis=0) - diag_val * diag_val) / (
        2.0 * off_weight
    ) + diag_val * (1.0 + diag_val / 2.0)
    back = jnp.dot(second_perm, grad_t, preferred_element_type=jnp.float32)
    result = (back - first.astype(jnp.float32) * scale_sum[None, :]) * inv_std0
    return result.astype(jnp.bfloat16)


def solution(mesh):
    x, y, c = (4, 8, 2)
    sub = Mesh(mesh.devices.reshape(x, y, c, mesh.devices.shape[1]), DP + ("mp",))
    return jax.shard_map(
        shards,
        mesh=sub,
        in_specs=(P(None, DP, None), P(None, "mp")),
        out_specs=P(DP, "mp"),
        check_vma=False,
    )
```

```python
import jax
import jax.numpy as jnp
from jax import lax
from jax.sharding import Mesh
from jax.sharding import PartitionSpec as P

off_weight = 0.0051
eps = 1e-05
DP = ("x", "y", "c")


def shift(v, axis, n, step):
    return lax.ppermute(v, axis, [(i, (i + step) % n) for i in range(n)])


def direct_gather(v, axis):
    n = lax.axis_size(axis)
    got = {0: v}
    for t in range(1, n):
        got[t] = lax.ppermute(v, axis, [(i, (i - t) % n) for i in range(n)])
    return jnp.stack([got[t] for t in range(n)])


def ring_gather(v, axis):
    n = lax.axis_size(axis)
    if n == 1:
        return v[None]
    right = n // 2
    left = n - 1 - right
    got = {0: v}
    cur = v
    for s in range(1, right + 1):
        cur = shift(cur, axis, n, 1)
        got[n - s] = cur
    cur = v
    for s in range(1, left + 1):
        cur = shift(cur, axis, n, -1)
        got[s] = cur
    return jnp.stack([got[t] for t in range(n)])


def dp_ring_gather(v):
    return ring_gather(ring_gather(direct_gather(v, "x"), "y"), "c")


def combine(mean, m2, count, axis, k):
    n = lax.axis_size(axis)
    pairs = [(i, i ^ k) for i in range(n)]
    other = lax.ppermute(jnp.stack([mean, m2]), axis, pairs)
    other_mean, other_m2 = other[0], other[1]
    delta = other_mean - mean
    new_mean = (mean + other_mean) * 0.5
    new_m2 = (m2 + other_m2) + delta * delta * (count * 0.5)
    return new_mean, new_m2, count * 2


def combine_all(mean, m2, count, axis):
    n = lax.axis_size(axis)
    got = jnp.roll(direct_gather(jnp.stack([mean, m2]), axis), lax.axis_index(axis), axis=0)
    means = [got[j, 0] for j in range(n)]
    m2s = [got[j, 1] for j in range(n)]
    while len(means) > 1:
        new_means, new_m2s = [], []
        for a in range(0, len(means), 2):
            delta = means[a + 1] - means[a]
            new_means.append((means[a] + means[a + 1]) * 0.5)
            new_m2s.append((m2s[a] + m2s[a + 1]) + delta * delta * (count * 0.5))
        means, m2s, count = new_means, new_m2s, count * 2
    return means[0], m2s[0], count


def dp_stats(feats):
    local = feats.shape[1]
    mean = jnp.sum(feats, axis=1, keepdims=True) / local
    dev = feats - mean
    m2 = jnp.sum(dev * dev, axis=1, keepdims=True)
    count = float(local)
    for axis in ("c", "y"):
        k = 1
        while k < lax.axis_size(axis):
            mean, m2, count = combine(mean, m2, count, axis, k)
            k *= 2
    mean, m2, count = combine_all(mean, m2, count, "x")
    return mean, m2 / count


def relative_order(v, axes):
    for dim, axis in enumerate(axes, start=1):
        v = jnp.roll(v, -lax.axis_index(axis), axis=dim)
    return v


def shards(hidden, proj_weight):
    mp_index = lax.axis_index("mp")
    dp_index = lax.axis_index(DP)
    dp_count = lax.axis_size(DP)
    nx, ny, nc = lax.axis_size("x"), lax.axis_size("y"), lax.axis_size("c")
    ix, iy, ic = lax.axis_index("x"), lax.axis_index("y"), lax.axis_index("c")
    rows = proj_weight.shape[1]
    local = hidden.shape[1]
    total = local * dp_count
    feats = jnp.einsum("vbh,hc->vbc", hidden, proj_weight, preferred_element_type=jnp.float32)
    feats0_all = lax.all_gather(feats[0], DP, axis=0, tiled=True)
    mean0 = jnp.sum(feats0_all, axis=0, keepdims=True) / total
    centered0 = feats0_all - mean0
    var0 = jnp.sum(centered0 * centered0, axis=0, keepdims=True) / total
    first_all = (centered0 / jnp.sqrt(var0 + eps)).astype(jnp.bfloat16)
    first = ((feats[0] - mean0) / jnp.sqrt(var0 + eps)).astype(jnp.bfloat16)
    inv_std0 = 1.0 / jnp.sqrt(var0 + eps)
    mean1, var1 = dp_stats(feats[1:])
    second = ((feats[1] - mean1[0]) / jnp.sqrt(var1[0] + eps)).astype(jnp.bfloat16)
    n_mp = lax.axis_size("mp")
    stacked = lax.all_gather(second, "mp", axis=0)
    second_full = jnp.transpose(stacked, (1, 0, 2)).reshape(local, n_mp * rows)
    width = second_full.shape[1] // dp_count
    columns = lax.all_to_all(second_full, DP, split_axis=1, concat_axis=0, tiled=True)
    second_perm = relative_order(second_full.reshape(local, nx, ny, nc, width), ("x", "y", "c"))
    second_perm = jnp.transpose(second_perm, (0, 3, 2, 1, 4)).reshape(local, dp_count * width)
    columns, second_perm = lax.optimization_barrier((columns, second_perm))
    corr = (
        jnp.einsum("bi,bj->ij", first_all, columns, preferred_element_type=jnp.float32)
        / total
    )
    row_ids = mp_index * rows + lax.iota(jnp.int32, rows)[:, None]
    col_ids = dp_index * width + lax.iota(jnp.int32, width)[None, :]
    grad_block = jnp.where(row_ids == col_ids, 2.0 * (corr - 1.0), 2.0 * off_weight * corr).astype(
        jnp.bfloat16
    )
    grad_t = dp_ring_gather(grad_block.T).reshape(dp_count * width, rows)
    t = lax.iota(jnp.int32, width)
    cc = (lax.iota(jnp.int32, nc) + ic) % nc
    yy = (lax.iota(jnp.int32, ny) + iy) % ny
    xx = (lax.iota(jnp.int32, nx) + ix) % nx
    perm_cols = (
        ((xx[None, None, :, None] * ny + yy[None, :, None, None]) * nc + cc[:, None, None, None]) * width
        + t[None, None, None, :]
    ).reshape(-1)
    grad_wide = grad_t.astype(jnp.float32)
    row_flat = mp_index * rows + lax.iota(jnp.int32, rows)
    diag_val = jnp.sum(jnp.where(perm_cols[:, None] == row_flat[None, :], grad_wide, 0.0), axis=0)
    scale_sum = (jnp.sum(grad_wide * grad_wide, axis=0) - diag_val * diag_val) / (
        2.0 * off_weight
    ) + diag_val * (1.0 + diag_val / 2.0)
    back = jnp.dot(second_perm, grad_t, preferred_element_type=jnp.float32)
    result = (back - first.astype(jnp.float32) * scale_sum[None, :]) * inv_std0
    return result.astype(jnp.bfloat16)


def solution(mesh):
    x, y, c = (4, 8, 2)
    sub = Mesh(mesh.devices.reshape(x, y, c, mesh.devices.shape[1]), DP + ("mp",))
    return jax.shard_map(
        shards,
        mesh=sub,
        in_specs=(P(None, DP, None), P(None, "mp")),
        out_specs=P(DP, "mp"),
        check_vma=False,
    )
```

```python
import jax
import jax.numpy as jnp
from jax import lax
from jax.sharding import Mesh
from jax.sharding import PartitionSpec as P

off_weight = 0.0051
eps = 1e-05
DP = ("x", "y", "c")


def shift(v, axis, n, step):
    return lax.ppermute(v, axis, [(i, (i + step) % n) for i in range(n)])


def direct_gather(v, axis):
    n = lax.axis_size(axis)
    got = {0: v}
    for t in range(1, n):
        got[t] = lax.ppermute(v, axis, [(i, (i - t) % n) for i in range(n)])
    return jnp.stack([got[t] for t in range(n)])


def ring_gather(v, axis):
    n = lax.axis_size(axis)
    if n == 1:
        return v[None]
    right = n // 2
    left = n - 1 - right
    got = {0: v}
    cur = v
    for s in range(1, right + 1):
        cur = shift(cur, axis, n, 1)
        got[n - s] = cur
    cur = v
    for s in range(1, left + 1):
        cur = shift(cur, axis, n, -1)
        got[s] = cur
    return jnp.stack([got[t] for t in range(n)])


def dp_ring_gather(v):
    return ring_gather(ring_gather(direct_gather(v, "x"), "y"), "c")


def combine(mean, m2, count, axis, k):
    n = lax.axis_size(axis)
    pairs = [(i, i ^ k) for i in range(n)]
    other = lax.ppermute(jnp.stack([mean, m2]), axis, pairs)
    other_mean, other_m2 = other[0], other[1]
    delta = other_mean - mean
    new_mean = (mean + other_mean) * 0.5
    new_m2 = (m2 + other_m2) + delta * delta * (count * 0.5)
    return new_mean, new_m2, count * 2


def combine_all(mean, m2, count, axis):
    n = lax.axis_size(axis)
    got = jnp.roll(direct_gather(jnp.stack([mean, m2]), axis), lax.axis_index(axis), axis=0)
    means = [got[j, 0] for j in range(n)]
    m2s = [got[j, 1] for j in range(n)]
    while len(means) > 1:
        new_means, new_m2s = [], []
        for a in range(0, len(means), 2):
            delta = means[a + 1] - means[a]
            new_means.append((means[a] + means[a + 1]) * 0.5)
            new_m2s.append((m2s[a] + m2s[a + 1]) + delta * delta * (count * 0.5))
        means, m2s, count = new_means, new_m2s, count * 2
    return means[0], m2s[0], count


def dp_stats(feats):
    local = feats.shape[1]
    mean = jnp.sum(feats, axis=1, keepdims=True) / local
    dev = feats - mean
    m2 = jnp.sum(dev * dev, axis=1, keepdims=True)
    count = float(local)
    for axis in ("c", "y"):
        k = 1
        while k < lax.axis_size(axis):
            mean, m2, count = combine(mean, m2, count, axis, k)
            k *= 2
    mean, m2, count = combine_all(mean, m2, count, "x")
    return mean, m2 / count


def relative_order(v, axes):
    for dim, axis in enumerate(axes, start=1):
        v = jnp.roll(v, -lax.axis_index(axis), axis=dim)
    return v


def shards(hidden, proj_weight):
    mp_index = lax.axis_index("mp")
    dp_index = lax.axis_index(DP)
    dp_count = lax.axis_size(DP)
    nx, ny, nc = lax.axis_size("x"), lax.axis_size("y"), lax.axis_size("c")
    ix, iy, ic = lax.axis_index("x"), lax.axis_index("y"), lax.axis_index("c")
    rows = proj_weight.shape[1]
    local = hidden.shape[1]
    total = local * dp_count
    feats = jnp.einsum("vbh,hc->vbc", hidden, proj_weight, preferred_element_type=jnp.float32)
    mean, var = dp_stats(feats)
    inv_std = 1.0 / jnp.sqrt(var + eps)
    feats0_all = lax.all_gather(feats[0], DP, axis=0, tiled=True)
    first_all = ((feats0_all - mean[0]) / jnp.sqrt(var[0] + eps)).astype(jnp.bfloat16)
    first = ((feats[0] - mean[0]) / jnp.sqrt(var[0] + eps)).astype(jnp.bfloat16)
    inv_std0 = inv_std[0]
    second = ((feats[1] - mean[1]) / jnp.sqrt(var[1] + eps)).astype(jnp.bfloat16)
    n_mp = lax.axis_size("mp")
    stacked = lax.all_gather(second, "mp", axis=0)
    second_full = jnp.transpose(stacked, (1, 0, 2)).reshape(local, n_mp * rows)
    width = second_full.shape[1] // dp_count
    columns = lax.all_to_all(second_full, DP, split_axis=1, concat_axis=0, tiled=True)
    second_perm = relative_order(second_full.reshape(local, nx, ny, nc, width), ("x", "y", "c"))
    second_perm = jnp.transpose(second_perm, (0, 3, 2, 1, 4)).reshape(local, dp_count * width)
    columns, second_perm = lax.optimization_barrier((columns, second_perm))
    corr = (
        jnp.einsum("bi,bj->ij", first_all, columns, preferred_element_type=jnp.float32)
        / total
    )
    row_ids = mp_index * rows + lax.iota(jnp.int32, rows)[:, None]
    col_ids = dp_index * width + lax.iota(jnp.int32, width)[None, :]
    grad_block = jnp.where(row_ids == col_ids, 2.0 * (corr - 1.0), 2.0 * off_weight * corr).astype(
        jnp.bfloat16
    )
    grad_t = dp_ring_gather(grad_block.T).reshape(dp_count * width, rows)
    t = lax.iota(jnp.int32, width)
    cc = (lax.iota(jnp.int32, nc) + ic) % nc
    yy = (lax.iota(jnp.int32, ny) + iy) % ny
    xx = (lax.iota(jnp.int32, nx) + ix) % nx
    perm_cols = (
        ((xx[None, None, :, None] * ny + yy[None, :, None, None]) * nc + cc[:, None, None, None]) * width
        + t[None, None, None, :]
    ).reshape(-1)
    grad_wide = grad_t.astype(jnp.float32)
    row_flat = mp_index * rows + lax.iota(jnp.int32, rows)
    diag_val = jnp.sum(jnp.where(perm_cols[:, None] == row_flat[None, :], grad_wide, 0.0), axis=0)
    scale_sum = (jnp.sum(grad_wide * grad_wide, axis=0) - diag_val * diag_val) / (
        2.0 * off_weight
    ) + diag_val * (1.0 + diag_val / 2.0)
    back = jnp.dot(second_perm, grad_t, preferred_element_type=jnp.float32)
    result = (back - first.astype(jnp.float32) * scale_sum[None, :]) * inv_std0
    return result.astype(jnp.bfloat16)


def solution(mesh):
    x, y, c = (4, 8, 2)
    sub = Mesh(mesh.devices.reshape(x, y, c, mesh.devices.shape[1]), DP + ("mp",))
    return jax.shard_map(
        shards,
        mesh=sub,
        in_specs=(P(None, DP, None), P(None, "mp")),
        out_specs=P(DP, "mp"),
        check_vma=False,
    )
```

```python
import jax
import jax.numpy as jnp
from jax import lax
from jax.sharding import Mesh
from jax.sharding import PartitionSpec as P

off_weight = 0.0051
eps = 1e-05
DP = ("x", "y", "c")


def shift(v, axis, n, step):
    return lax.ppermute(v, axis, [(i, (i + step) % n) for i in range(n)])


def direct_gather(v, axis):
    n = lax.axis_size(axis)
    got = {0: v}
    for t in range(1, n):
        got[t] = lax.ppermute(v, axis, [(i, (i - t) % n) for i in range(n)])
    return jnp.stack([got[t] for t in range(n)])


def ring_gather(v, axis):
    n = lax.axis_size(axis)
    if n == 1:
        return v[None]
    right = n // 2
    left = n - 1 - right
    got = {0: v}
    cur = v
    for s in range(1, right + 1):
        cur = shift(cur, axis, n, 1)
        got[n - s] = cur
    cur = v
    for s in range(1, left + 1):
        cur = shift(cur, axis, n, -1)
        got[s] = cur
    return jnp.stack([got[t] for t in range(n)])


def dp_ring_gather(v):
    return ring_gather(ring_gather(direct_gather(v, "x"), "y"), "c")


def combine(mean, m2, count, axis, k):
    n = lax.axis_size(axis)
    pairs = [(i, i ^ k) for i in range(n)]
    other = lax.ppermute(jnp.stack([mean, m2]), axis, pairs)
    other_mean, other_m2 = other[0], other[1]
    delta = other_mean - mean
    new_mean = (mean + other_mean) * 0.5
    new_m2 = (m2 + other_m2) + delta * delta * (count * 0.5)
    return new_mean, new_m2, count * 2


def combine_all(mean, m2, count, axis):
    n = lax.axis_size(axis)
    got = jnp.roll(direct_gather(jnp.stack([mean, m2]), axis), lax.axis_index(axis), axis=0)
    means = [got[j, 0] for j in range(n)]
    m2s = [got[j, 1] for j in range(n)]
    while len(means) > 1:
        new_means, new_m2s = [], []
        for a in range(0, len(means), 2):
            delta = means[a + 1] - means[a]
            new_means.append((means[a] + means[a + 1]) * 0.5)
            new_m2s.append((m2s[a] + m2s[a + 1]) + delta * delta * (count * 0.5))
        means, m2s, count = new_means, new_m2s, count * 2
    return means[0], m2s[0], count


def dp_stats(feats):
    local = feats.shape[1]
    mean = jnp.sum(feats, axis=1, keepdims=True) / local
    dev = feats - mean
    m2 = jnp.sum(dev * dev, axis=1, keepdims=True)
    count = float(local)
    for axis in ("c", "y"):
        k = 1
        while k < lax.axis_size(axis):
            mean, m2, count = combine(mean, m2, count, axis, k)
            k *= 2
    mean, m2, count = combine_all(mean, m2, count, "x")
    return mean, m2 / count


def relative_order(v, axes):
    for dim, axis in enumerate(axes, start=1):
        v = jnp.roll(v, -lax.axis_index(axis), axis=dim)
    return v


def shards(hidden, proj_weight):
    mp_index = lax.axis_index("mp")
    dp_index = lax.axis_index(DP)
    dp_count = lax.axis_size(DP)
    nx, ny, nc = lax.axis_size("x"), lax.axis_size("y"), lax.axis_size("c")
    ix, iy, ic = lax.axis_index("x"), lax.axis_index("y"), lax.axis_index("c")
    rows = proj_weight.shape[1]
    local = hidden.shape[1]
    total = local * dp_count
    feats = jnp.einsum("vbh,hc->vbc", hidden, proj_weight, preferred_element_type=jnp.float32)
    feats0_all = lax.all_gather(feats[0], DP, axis=0, tiled=True)
    mean0 = jnp.sum(feats0_all, axis=0, keepdims=True) / total
    centered0 = feats0_all - mean0
    var0 = jnp.sum(centered0 * centered0, axis=0, keepdims=True) / total
    first_all = (centered0 / jnp.sqrt(var0 + eps)).astype(jnp.bfloat16)
    first = ((feats[0] - mean0) / jnp.sqrt(var0 + eps)).astype(jnp.bfloat16)
    inv_std0 = 1.0 / jnp.sqrt(var0 + eps)
    mean1, var1 = dp_stats(feats[1:])
    second = ((feats[1] - mean1[0]) / jnp.sqrt(var1[0] + eps)).astype(jnp.bfloat16)
    n_mp = lax.axis_size("mp")
    stacked = lax.all_gather(second, "mp", axis=0)
    second_full = jnp.transpose(stacked, (1, 0, 2)).reshape(local, n_mp * rows)
    width = second_full.shape[1] // dp_count
    columns = lax.all_to_all(second_full, DP, split_axis=1, concat_axis=0, tiled=True)
    second_perm = relative_order(second_full.reshape(local, nx, ny, nc, width), ("x", "y", "c"))
    second_perm = jnp.transpose(second_perm, (0, 3, 2, 1, 4)).reshape(local, dp_count * width)
    columns, second_perm = lax.optimization_barrier((columns, second_perm))
    corr = (
        jnp.einsum("bi,bj->ij", first_all, columns, preferred_element_type=jnp.float32)
        / total
    )
    row_ids = mp_index * rows + lax.iota(jnp.int32, rows)[:, None]
    col_ids = dp_index * width + lax.iota(jnp.int32, width)[None, :]
    grad_block = jnp.where(row_ids == col_ids, 2.0 * (corr - 1.0), 2.0 * off_weight * corr).astype(
        jnp.bfloat16
    )
    own = ring_gather(direct_gather(grad_block.T, "x"), "y")
    other = shift(own, "c", nc, 1)
    half = ny * nx * width
    t = lax.iota(jnp.int32, width)
    yy = (lax.iota(jnp.int32, ny) + iy) % ny
    xx = (lax.iota(jnp.int32, nx) + ix) % nx
    row_flat = mp_index * rows + lax.iota(jnp.int32, rows)
    back = None
    sq_sum = None
    diag_val = None
    for k, part in enumerate((own, other)):
        cc = (ic + k) % nc
        perm_cols = (((xx[None, :, None] * ny + yy[:, None, None]) * nc + cc) * width + t[None, None, :]).reshape(-1)
        g = part.reshape(half, rows)
        g_wide = g.astype(jnp.float32)
        d = jnp.sum(jnp.where(perm_cols[:, None] == row_flat[None, :], g_wide, 0.0), axis=0)
        q = jnp.sum(g_wide * g_wide, axis=0)
        b = jnp.dot(second_perm[:, k * half:(k + 1) * half], g, preferred_element_type=jnp.float32)
        back = b if back is None else back + b
        sq_sum = q if sq_sum is None else sq_sum + q
        diag_val = d if diag_val is None else diag_val + d
    scale_sum = (sq_sum - diag_val * diag_val) / (2.0 * off_weight) + diag_val * (1.0 + diag_val / 2.0)
    result = (back - first.astype(jnp.float32) * scale_sum[None, :]) * inv_std0
    return result.astype(jnp.bfloat16)


def solution(mesh):
    x, y, c = (4, 8, 2)
    sub = Mesh(mesh.devices.reshape(x, y, c, mesh.devices.shape[1]), DP + ("mp",))
    return jax.shard_map(
        shards,
        mesh=sub,
        in_specs=(P(None, DP, None), P(None, "mp")),
        out_specs=P(DP, "mp"),
        check_vma=False,
    )
```

```python
import jax
import jax.numpy as jnp
from jax import lax
from jax.sharding import Mesh
from jax.sharding import PartitionSpec as P

off_weight = 0.0051
eps = 1e-05
DP = ("x", "y", "c")


def shift(v, axis, n, step):
    return lax.ppermute(v, axis, [(i, (i + step) % n) for i in range(n)])


def direct_gather(v, axis):
    n = lax.axis_size(axis)
    got = {0: v}
    for t in range(1, n):
        got[t] = lax.ppermute(v, axis, [(i, (i - t) % n) for i in range(n)])
    return jnp.stack([got[t] for t in range(n)])


def ring_gather(v, axis):
    n = lax.axis_size(axis)
    if n == 1:
        return v[None]
    right = n // 2
    left = n - 1 - right
    got = {0: v}
    cur = v
    for s in range(1, right + 1):
        cur = shift(cur, axis, n, 1)
        got[n - s] = cur
    cur = v
    for s in range(1, left + 1):
        cur = shift(cur, axis, n, -1)
        got[s] = cur
    return jnp.stack([got[t] for t in range(n)])


def dp_ring_gather(v):
    return ring_gather(ring_gather(direct_gather(v, "x"), "y"), "c")


def combine(mean, m2, count, axis, k):
    n = lax.axis_size(axis)
    pairs = [(i, i ^ k) for i in range(n)]
    other = lax.ppermute(jnp.stack([mean, m2]), axis, pairs)
    other_mean, other_m2 = other[0], other[1]
    delta = other_mean - mean
    new_mean = (mean + other_mean) * 0.5
    new_m2 = (m2 + other_m2) + delta * delta * (count * 0.5)
    return new_mean, new_m2, count * 2


def combine_all(mean, m2, count, axis):
    n = lax.axis_size(axis)
    got = jnp.roll(direct_gather(jnp.stack([mean, m2]), axis), lax.axis_index(axis), axis=0)
    means = [got[j, 0] for j in range(n)]
    m2s = [got[j, 1] for j in range(n)]
    while len(means) > 1:
        new_means, new_m2s = [], []
        for a in range(0, len(means), 2):
            delta = means[a + 1] - means[a]
            new_means.append((means[a] + means[a + 1]) * 0.5)
            new_m2s.append((m2s[a] + m2s[a + 1]) + delta * delta * (count * 0.5))
        means, m2s, count = new_means, new_m2s, count * 2
    return means[0], m2s[0], count


def dp_stats(feats):
    local = feats.shape[1]
    mean = jnp.sum(feats, axis=1, keepdims=True) / local
    dev = feats - mean
    m2 = jnp.sum(dev * dev, axis=1, keepdims=True)
    count = float(local)
    for axis in ("c", "y"):
        k = 1
        while k < lax.axis_size(axis):
            mean, m2, count = combine(mean, m2, count, axis, k)
            k *= 2
    mean, m2, count = combine_all(mean, m2, count, "x")
    return mean, m2 / count


def shards(hidden, proj_weight):
    mp_index = lax.axis_index("mp")
    dp_index = lax.axis_index(DP)
    dp_count = lax.axis_size(DP)
    nx, ny, nc = lax.axis_size("x"), lax.axis_size("y"), lax.axis_size("c")
    ix, iy, ic = lax.axis_index("x"), lax.axis_index("y"), lax.axis_index("c")
    rows = proj_weight.shape[1]
    local = hidden.shape[1]
    total = local * dp_count
    feats = jnp.einsum("vbh,hc->vbc", hidden, proj_weight, preferred_element_type=jnp.float32)
    feats0_all = lax.all_gather(feats[0], DP, axis=0, tiled=True)
    mean0 = jnp.sum(feats0_all, axis=0, keepdims=True) / total
    centered0 = feats0_all - mean0
    var0 = jnp.sum(centered0 * centered0, axis=0, keepdims=True) / total
    first_all = (centered0 / jnp.sqrt(var0 + eps)).astype(jnp.bfloat16)
    first = ((feats[0] - mean0) / jnp.sqrt(var0 + eps)).astype(jnp.bfloat16)
    inv_std0 = 1.0 / jnp.sqrt(var0 + eps)
    mean1, var1 = dp_stats(feats[1:])
    second = ((feats[1] - mean1[0]) / jnp.sqrt(var1[0] + eps)).astype(jnp.bfloat16)
    n_mp = lax.axis_size("mp")
    stacked = lax.all_gather(second, "mp", axis=0)
    second_full = jnp.transpose(stacked, (1, 0, 2)).reshape(local, n_mp * rows)
    width = second_full.shape[1] // dp_count
    columns = lax.all_to_all(second_full, DP, split_axis=1, concat_axis=0, tiled=True)
    pc = (lax.iota(jnp.int32, nc)[:, None, None] + ic) % nc
    py = (lax.iota(jnp.int32, ny)[None, :, None] + iy) % ny
    px = (lax.iota(jnp.int32, nx)[None, None, :] + ix) % nx
    src_block = ((px * ny + py) * nc + pc).reshape(-1)
    pick = (src_block[:, None] == lax.iota(jnp.int32, dp_count)[None, :]).astype(jnp.bfloat16)
    second_perm = jnp.einsum(
        "bkt,pk->bpt", second_full.reshape(local, dp_count, width), pick, preferred_element_type=jnp.float32
    ).astype(jnp.bfloat16).reshape(local, dp_count * width)
    columns, second_perm = lax.optimization_barrier((columns, second_perm))
    corr = (
        jnp.einsum("bi,bj->ij", first_all, columns, preferred_element_type=jnp.float32)
        / total
    )
    row_ids = mp_index * rows + lax.iota(jnp.int32, rows)[:, None]
    col_ids = dp_index * width + lax.iota(jnp.int32, width)[None, :]
    grad_block = jnp.where(row_ids == col_ids, 2.0 * (corr - 1.0), 2.0 * off_weight * corr).astype(
        jnp.bfloat16
    )
    grad_t = dp_ring_gather(grad_block.T).reshape(dp_count * width, rows)
    t = lax.iota(jnp.int32, width)
    cc = (lax.iota(jnp.int32, nc) + ic) % nc
    yy = (lax.iota(jnp.int32, ny) + iy) % ny
    xx = (lax.iota(jnp.int32, nx) + ix) % nx
    perm_cols = (
        ((xx[None, None, :, None] * ny + yy[None, :, None, None]) * nc + cc[:, None, None, None]) * width
        + t[None, None, None, :]
    ).reshape(-1)
    grad_wide = grad_t.astype(jnp.float32)
    row_flat = mp_index * rows + lax.iota(jnp.int32, rows)
    diag_val = jnp.sum(jnp.where(perm_cols[:, None] == row_flat[None, :], grad_wide, 0.0), axis=0)
    scale_sum = (jnp.sum(grad_wide * grad_wide, axis=0) - diag_val * diag_val) / (
        2.0 * off_weight
    ) + diag_val * (1.0 + diag_val / 2.0)
    back = jnp.dot(second_perm, grad_t, preferred_element_type=jnp.float32)
    result = (back - first.astype(jnp.float32) * scale_sum[None, :]) * inv_std0
    return result.astype(jnp.bfloat16)


def solution(mesh):
    x, y, c = (4, 8, 2)
    sub = Mesh(mesh.devices.reshape(x, y, c, mesh.devices.shape[1]), DP + ("mp",))
    return jax.shard_map(
        shards,
        mesh=sub,
        in_specs=(P(None, DP, None), P(None, "mp")),
        out_specs=P(DP, "mp"),
        check_vma=False,
    )
```

```python
import jax
import jax.numpy as jnp
from jax import lax
from jax.sharding import Mesh
from jax.sharding import PartitionSpec as P

off_weight = 0.0051
eps = 1e-05
DP = ("x", "y", "c")


def shift(v, axis, n, step):
    return lax.ppermute(v, axis, [(i, (i + step) % n) for i in range(n)])


def direct_gather(v, axis):
    n = lax.axis_size(axis)
    got = {0: v}
    for t in range(1, n):
        got[t] = lax.ppermute(v, axis, [(i, (i - t) % n) for i in range(n)])
    return jnp.stack([got[t] for t in range(n)])


def ring_gather(v, axis):
    n = lax.axis_size(axis)
    if n == 1:
        return v[None]
    right = n // 2
    left = n - 1 - right
    got = {0: v}
    cur = v
    for s in range(1, right + 1):
        cur = shift(cur, axis, n, 1)
        got[n - s] = cur
    cur = v
    for s in range(1, left + 1):
        cur = shift(cur, axis, n, -1)
        got[s] = cur
    return jnp.stack([got[t] for t in range(n)])


def dp_ring_gather(v):
    return ring_gather(ring_gather(direct_gather(v, "x"), "y"), "c")


def combine(mean, m2, count, axis, k):
    n = lax.axis_size(axis)
    pairs = [(i, i ^ k) for i in range(n)]
    other = lax.ppermute(jnp.stack([mean, m2]), axis, pairs)
    other_mean, other_m2 = other[0], other[1]
    delta = other_mean - mean
    new_mean = (mean + other_mean) * 0.5
    new_m2 = (m2 + other_m2) + delta * delta * (count * 0.5)
    return new_mean, new_m2, count * 2


def combine_all(mean, m2, count, axis):
    n = lax.axis_size(axis)
    got = jnp.roll(direct_gather(jnp.stack([mean, m2]), axis), lax.axis_index(axis), axis=0)
    means = [got[j, 0] for j in range(n)]
    m2s = [got[j, 1] for j in range(n)]
    while len(means) > 1:
        new_means, new_m2s = [], []
        for a in range(0, len(means), 2):
            delta = means[a + 1] - means[a]
            new_means.append((means[a] + means[a + 1]) * 0.5)
            new_m2s.append((m2s[a] + m2s[a + 1]) + delta * delta * (count * 0.5))
        means, m2s, count = new_means, new_m2s, count * 2
    return means[0], m2s[0], count


def dp_stats(feats):
    local = feats.shape[1]
    mean = jnp.sum(feats, axis=1, keepdims=True) / local
    dev = feats - mean
    m2 = jnp.sum(dev * dev, axis=1, keepdims=True)
    count = float(local)
    for axis in ("c", "y"):
        k = 1
        while k < lax.axis_size(axis):
            mean, m2, count = combine(mean, m2, count, axis, k)
            k *= 2
    mean, m2, count = combine_all(mean, m2, count, "x")
    return mean, m2 / count


def shards(hidden, proj_weight):
    mp_index = lax.axis_index("mp")
    dp_index = lax.axis_index(DP)
    dp_count = lax.axis_size(DP)
    nx, ny, nc = lax.axis_size("x"), lax.axis_size("y"), lax.axis_size("c")
    ix, iy, ic = lax.axis_index("x"), lax.axis_index("y"), lax.axis_index("c")
    rows = proj_weight.shape[1]
    local = hidden.shape[1]
    total = local * dp_count
    feats = jnp.einsum("vbh,hc->vbc", hidden, proj_weight, preferred_element_type=jnp.float32)
    feats0_all = lax.all_gather(feats[0], DP, axis=0, tiled=True)
    mean0 = jnp.sum(feats0_all, axis=0, keepdims=True) / total
    centered0 = feats0_all - mean0
    var0 = jnp.sum(centered0 * centered0, axis=0, keepdims=True) / total
    first_all = (centered0 / jnp.sqrt(var0 + eps)).astype(jnp.bfloat16)
    first = ((feats[0] - mean0) / jnp.sqrt(var0 + eps)).astype(jnp.bfloat16)
    inv_std0 = 1.0 / jnp.sqrt(var0 + eps)
    mean1, var1 = dp_stats(feats[1:])
    second = ((feats[1] - mean1[0]) / jnp.sqrt(var1[0] + eps)).astype(jnp.bfloat16)
    n_mp = lax.axis_size("mp")
    stacked = lax.all_gather(second, "mp", axis=0)
    second_full = jnp.transpose(stacked, (1, 0, 2)).reshape(local, n_mp * rows)
    width = second_full.shape[1] // dp_count
    columns = lax.all_to_all(second_full, DP, split_axis=1, concat_axis=0, tiled=True)
    pc = (lax.iota(jnp.int32, nc)[:, None, None] + ic) % nc
    py = (lax.iota(jnp.int32, ny)[None, :, None] + iy) % ny
    px = (lax.iota(jnp.int32, nx)[None, None, :] + ix) % nx
    src_block = ((px * ny + py) * nc + pc).reshape(-1)
    pick = (src_block[:, None] == lax.iota(jnp.int32, dp_count)[None, :]).astype(jnp.bfloat16)
    first_all, reorder_in = lax.optimization_barrier((first_all, second_full))
    second_perm = jnp.einsum(
        "bkt,pk->bpt", reorder_in.reshape(local, dp_count, width), pick, preferred_element_type=jnp.float32
    ).astype(jnp.bfloat16).reshape(local, dp_count * width)
    columns, second_perm = lax.optimization_barrier((columns, second_perm))
    corr = (
        jnp.einsum("bi,bj->ij", first_all, columns, preferred_element_type=jnp.float32)
        / total
    )
    row_ids = mp_index * rows + lax.iota(jnp.int32, rows)[:, None]
    col_ids = dp_index * width + lax.iota(jnp.int32, width)[None, :]
    grad_block = jnp.where(row_ids == col_ids, 2.0 * (corr - 1.0), 2.0 * off_weight * corr).astype(
        jnp.bfloat16
    )
    grad_t = dp_ring_gather(grad_block.T).reshape(dp_count * width, rows)
    t = lax.iota(jnp.int32, width)
    cc = (lax.iota(jnp.int32, nc) + ic) % nc
    yy = (lax.iota(jnp.int32, ny) + iy) % ny
    xx = (lax.iota(jnp.int32, nx) + ix) % nx
    perm_cols = (
        ((xx[None, None, :, None] * ny + yy[None, :, None, None]) * nc + cc[:, None, None, None]) * width
        + t[None, None, None, :]
    ).reshape(-1)
    grad_wide = grad_t.astype(jnp.float32)
    row_flat = mp_index * rows + lax.iota(jnp.int32, rows)
    diag_val = jnp.sum(jnp.where(perm_cols[:, None] == row_flat[None, :], grad_wide, 0.0), axis=0)
    scale_sum = (jnp.sum(grad_wide * grad_wide, axis=0) - diag_val * diag_val) / (
        2.0 * off_weight
    ) + diag_val * (1.0 + diag_val / 2.0)
    back = jnp.dot(second_perm, grad_t, preferred_element_type=jnp.float32)
    result = (back - first.astype(jnp.float32) * scale_sum[None, :]) * inv_std0
    return result.astype(jnp.bfloat16)


def solution(mesh):
    x, y, c = (4, 8, 2)
    sub = Mesh(mesh.devices.reshape(x, y, c, mesh.devices.shape[1]), DP + ("mp",))
    return jax.shard_map(
        shards,
        mesh=sub,
        in_specs=(P(None, DP, None), P(None, "mp")),
        out_specs=P(DP, "mp"),
        check_vma=False,
    )
```

```python
import jax
import jax.numpy as jnp
from jax import lax
from jax.sharding import Mesh
from jax.sharding import PartitionSpec as P

off_weight = 0.0051
eps = 1e-05
DP = ("x", "y", "c")


def shift(v, axis, n, step):
    return lax.ppermute(v, axis, [(i, (i + step) % n) for i in range(n)])


def direct_gather(v, axis):
    n = lax.axis_size(axis)
    got = {0: v}
    for t in range(1, n):
        got[t] = lax.ppermute(v, axis, [(i, (i - t) % n) for i in range(n)])
    return jnp.stack([got[t] for t in range(n)])


def ring_gather(v, axis):
    n = lax.axis_size(axis)
    if n == 1:
        return v[None]
    right = n // 2
    left = n - 1 - right
    got = {0: v}
    cur = v
    for s in range(1, right + 1):
        cur = shift(cur, axis, n, 1)
        got[n - s] = cur
    cur = v
    for s in range(1, left + 1):
        cur = shift(cur, axis, n, -1)
        got[s] = cur
    return jnp.stack([got[t] for t in range(n)])


def dp_ring_gather(v):
    return ring_gather(ring_gather(direct_gather(v, "x"), "y"), "c")


def combine(mean, m2, count, axis, k):
    n = lax.axis_size(axis)
    pairs = [(i, i ^ k) for i in range(n)]
    other = lax.ppermute(jnp.stack([mean, m2]), axis, pairs)
    other_mean, other_m2 = other[0], other[1]
    delta = other_mean - mean
    new_mean = (mean + other_mean) * 0.5
    new_m2 = (m2 + other_m2) + delta * delta * (count * 0.5)
    return new_mean, new_m2, count * 2


def combine_all(mean, m2, count, axis):
    n = lax.axis_size(axis)
    got = jnp.roll(direct_gather(jnp.stack([mean, m2]), axis), lax.axis_index(axis), axis=0)
    means = [got[j, 0] for j in range(n)]
    m2s = [got[j, 1] for j in range(n)]
    while len(means) > 1:
        new_means, new_m2s = [], []
        for a in range(0, len(means), 2):
            delta = means[a + 1] - means[a]
            new_means.append((means[a] + means[a + 1]) * 0.5)
            new_m2s.append((m2s[a] + m2s[a + 1]) + delta * delta * (count * 0.5))
        means, m2s, count = new_means, new_m2s, count * 2
    return means[0], m2s[0], count


def dp_stats(feats):
    local = feats.shape[1]
    mean = jnp.sum(feats, axis=1, keepdims=True) / local
    dev = feats - mean
    m2 = jnp.sum(dev * dev, axis=1, keepdims=True)
    count = float(local)
    for axis in ("c", "y"):
        k = 1
        while k < lax.axis_size(axis):
            mean, m2, count = combine(mean, m2, count, axis, k)
            k *= 2
    mean, m2, count = combine_all(mean, m2, count, "x")
    return mean, m2 / count


def shards(hidden, proj_weight):
    mp_index = lax.axis_index("mp")
    dp_index = lax.axis_index(DP)
    dp_count = lax.axis_size(DP)
    nx, ny, nc = lax.axis_size("x"), lax.axis_size("y"), lax.axis_size("c")
    ix, iy, ic = lax.axis_index("x"), lax.axis_index("y"), lax.axis_index("c")
    rows = proj_weight.shape[1]
    local = hidden.shape[1]
    total = local * dp_count
    feats = jnp.einsum("vbh,hc->vbc", hidden, proj_weight, preferred_element_type=jnp.float32)
    feats0_all = lax.all_gather(feats[0], DP, axis=0, tiled=True)
    mean0 = jnp.sum(feats0_all, axis=0, keepdims=True) / total
    centered0 = feats0_all - mean0
    var0 = jnp.sum(centered0 * centered0, axis=0, keepdims=True) / total
    first_all = (centered0 / jnp.sqrt(var0 + eps)).astype(jnp.bfloat16)
    first = ((feats[0] - mean0) / jnp.sqrt(var0 + eps)).astype(jnp.bfloat16)
    inv_std0 = 1.0 / jnp.sqrt(var0 + eps)
    mean1, var1 = dp_stats(feats[1:])
    second = ((feats[1] - mean1[0]) / jnp.sqrt(var1[0] + eps)).astype(jnp.bfloat16)
    n_mp = lax.axis_size("mp")
    stacked = lax.all_to_all(
        jnp.broadcast_to(second[None], (n_mp,) + second.shape), "mp", split_axis=0, concat_axis=0, tiled=True
    )
    second_full = jnp.transpose(stacked, (1, 0, 2)).reshape(local, n_mp * rows)
    width = second_full.shape[1] // dp_count
    columns = lax.all_to_all(second_full, DP, split_axis=1, concat_axis=0, tiled=True)
    pc = (lax.iota(jnp.int32, nc)[:, None, None] + ic) % nc
    py = (lax.iota(jnp.int32, ny)[None, :, None] + iy) % ny
    px = (lax.iota(jnp.int32, nx)[None, None, :] + ix) % nx
    src_block = ((px * ny + py) * nc + pc).reshape(-1)
    pick = (src_block[:, None] == lax.iota(jnp.int32, dp_count)[None, :]).astype(jnp.bfloat16)
    second_perm = jnp.einsum(
        "bkt,pk->bpt", second_full.reshape(local, dp_count, width), pick, preferred_element_type=jnp.float32
    ).astype(jnp.bfloat16).reshape(local, dp_count * width)
    columns, second_perm = lax.optimization_barrier((columns, second_perm))
    corr = (
        jnp.einsum("bi,bj->ij", first_all, columns, preferred_element_type=jnp.float32)
        / total
    )
    row_ids = mp_index * rows + lax.iota(jnp.int32, rows)[:, None]
    col_ids = dp_index * width + lax.iota(jnp.int32, width)[None, :]
    grad_block = jnp.where(row_ids == col_ids, 2.0 * (corr - 1.0), 2.0 * off_weight * corr).astype(
        jnp.bfloat16
    )
    grad_t = dp_ring_gather(grad_block.T).reshape(dp_count * width, rows)
    t = lax.iota(jnp.int32, width)
    cc = (lax.iota(jnp.int32, nc) + ic) % nc
    yy = (lax.iota(jnp.int32, ny) + iy) % ny
    xx = (lax.iota(jnp.int32, nx) + ix) % nx
    perm_cols = (
        ((xx[None, None, :, None] * ny + yy[None, :, None, None]) * nc + cc[:, None, None, None]) * width
        + t[None, None, None, :]
    ).reshape(-1)
    grad_wide = grad_t.astype(jnp.float32)
    row_flat = mp_index * rows + lax.iota(jnp.int32, rows)
    diag_val = jnp.sum(jnp.where(perm_cols[:, None] == row_flat[None, :], grad_wide, 0.0), axis=0)
    scale_sum = (jnp.sum(grad_wide * grad_wide, axis=0) - diag_val * diag_val) / (
        2.0 * off_weight
    ) + diag_val * (1.0 + diag_val / 2.0)
    back = jnp.dot(second_perm, grad_t, preferred_element_type=jnp.float32)
    result = (back - first.astype(jnp.float32) * scale_sum[None, :]) * inv_std0
    return result.astype(jnp.bfloat16)


def solution(mesh):
    x, y, c = (4, 8, 2)
    sub = Mesh(mesh.devices.reshape(x, y, c, mesh.devices.shape[1]), DP + ("mp",))
    return jax.shard_map(
        shards,
        mesh=sub,
        in_specs=(P(None, DP, None), P(None, "mp")),
        out_specs=P(DP, "mp"),
        check_vma=False,
    )
```

```python
import jax
import jax.numpy as jnp
from jax import lax
from jax.sharding import Mesh
from jax.sharding import PartitionSpec as P

off_weight = 0.0051
eps = 1e-05
DP = ("x", "y", "c")


def shift(v, axis, n, step):
    return lax.ppermute(v, axis, [(i, (i + step) % n) for i in range(n)])


def direct_gather(v, axis):
    n = lax.axis_size(axis)
    got = {0: v}
    for t in range(1, n):
        got[t] = lax.ppermute(v, axis, [(i, (i - t) % n) for i in range(n)])
    return jnp.stack([got[t] for t in range(n)])


def ring_gather(v, axis):
    n = lax.axis_size(axis)
    if n == 1:
        return v[None]
    right = n // 2
    left = n - 1 - right
    got = {0: v}
    cur = v
    for s in range(1, right + 1):
        cur = shift(cur, axis, n, 1)
        got[n - s] = cur
    cur = v
    for s in range(1, left + 1):
        cur = shift(cur, axis, n, -1)
        got[s] = cur
    return jnp.stack([got[t] for t in range(n)])


def dp_ring_gather(v):
    return ring_gather(ring_gather(direct_gather(v, "x"), "y"), "c")


def combine(mean, m2, count, axis, k):
    n = lax.axis_size(axis)
    pairs = [(i, i ^ k) for i in range(n)]
    other = lax.ppermute(jnp.stack([mean, m2]), axis, pairs)
    other_mean, other_m2 = other[0], other[1]
    delta = other_mean - mean
    new_mean = (mean + other_mean) * 0.5
    new_m2 = (m2 + other_m2) + delta * delta * (count * 0.5)
    return new_mean, new_m2, count * 2


def combine_all(mean, m2, count, axis):
    n = lax.axis_size(axis)
    got = jnp.roll(direct_gather(jnp.stack([mean, m2]), axis), lax.axis_index(axis), axis=0)
    means = [got[j, 0] for j in range(n)]
    m2s = [got[j, 1] for j in range(n)]
    while len(means) > 1:
        new_means, new_m2s = [], []
        for a in range(0, len(means), 2):
            delta = means[a + 1] - means[a]
            new_means.append((means[a] + means[a + 1]) * 0.5)
            new_m2s.append((m2s[a] + m2s[a + 1]) + delta * delta * (count * 0.5))
        means, m2s, count = new_means, new_m2s, count * 2
    return means[0], m2s[0], count


def dp_stats(feats):
    local = feats.shape[1]
    mean = jnp.sum(feats, axis=1, keepdims=True) / local
    dev = feats - mean
    m2 = jnp.sum(dev * dev, axis=1, keepdims=True)
    count = float(local)
    for axis in ("c", "y"):
        k = 1
        while k < lax.axis_size(axis):
            mean, m2, count = combine(mean, m2, count, axis, k)
            k *= 2
    mean, m2, count = combine_all(mean, m2, count, "x")
    return mean, m2 / count


def shards(hidden, proj_weight):
    mp_index = lax.axis_index("mp")
    dp_index = lax.axis_index(DP)
    dp_count = lax.axis_size(DP)
    nx, ny, nc = lax.axis_size("x"), lax.axis_size("y"), lax.axis_size("c")
    ix, iy, ic = lax.axis_index("x"), lax.axis_index("y"), lax.axis_index("c")
    rows = proj_weight.shape[1]
    local = hidden.shape[1]
    total = local * dp_count
    feats = jnp.einsum("vbh,hc->vbc", hidden, proj_weight, preferred_element_type=jnp.float32)
    feats0_all = lax.all_gather(feats[0], DP, axis=0, tiled=True)
    mean0 = jnp.sum(feats0_all, axis=0, keepdims=True) / total
    centered0 = feats0_all - mean0
    var0 = jnp.sum(centered0 * centered0, axis=0, keepdims=True) / total
    first_all = (centered0 / jnp.sqrt(var0 + eps)).astype(jnp.bfloat16)
    first = ((feats[0] - mean0) / jnp.sqrt(var0 + eps)).astype(jnp.bfloat16)
    inv_std0 = 1.0 / jnp.sqrt(var0 + eps)
    mean1, var1 = dp_stats(feats[1:])
    second = ((feats[1] - mean1[0]) / jnp.sqrt(var1[0] + eps)).astype(jnp.bfloat16)
    n_mp = lax.axis_size("mp")
    stacked = lax.all_gather(second, "mp", axis=0)
    second_full = jnp.transpose(stacked, (1, 0, 2)).reshape(local, n_mp * rows)
    width = second_full.shape[1] // dp_count
    chips = lax.all_to_all(second_full, ("x", "y"), split_axis=1, concat_axis=0, tiled=True)
    columns = lax.all_to_all(chips, "c", split_axis=1, concat_axis=0, tiled=True)
    columns = jnp.transpose(columns.reshape(nc, nx * ny, local, width), (1, 0, 2, 3)).reshape(total, width)
    pc = (lax.iota(jnp.int32, nc)[:, None, None] + ic) % nc
    py = (lax.iota(jnp.int32, ny)[None, :, None] + iy) % ny
    px = (lax.iota(jnp.int32, nx)[None, None, :] + ix) % nx
    src_block = ((px * ny + py) * nc + pc).reshape(-1)
    pick = (src_block[:, None] == lax.iota(jnp.int32, dp_count)[None, :]).astype(jnp.bfloat16)
    second_perm = jnp.einsum(
        "bkt,pk->bpt", second_full.reshape(local, dp_count, width), pick, preferred_element_type=jnp.float32
    ).astype(jnp.bfloat16).reshape(local, dp_count * width)
    columns, second_perm = lax.optimization_barrier((columns, second_perm))
    corr = (
        jnp.einsum("bi,bj->ij", first_all, columns, preferred_element_type=jnp.float32)
        / total
    )
    row_ids = mp_index * rows + lax.iota(jnp.int32, rows)[:, None]
    col_ids = dp_index * width + lax.iota(jnp.int32, width)[None, :]
    grad_block = jnp.where(row_ids == col_ids, 2.0 * (corr - 1.0), 2.0 * off_weight * corr).astype(
        jnp.bfloat16
    )
    grad_t = dp_ring_gather(grad_block.T).reshape(dp_count * width, rows)
    t = lax.iota(jnp.int32, width)
    cc = (lax.iota(jnp.int32, nc) + ic) % nc
    yy = (lax.iota(jnp.int32, ny) + iy) % ny
    xx = (lax.iota(jnp.int32, nx) + ix) % nx
    perm_cols = (
        ((xx[None, None, :, None] * ny + yy[None, :, None, None]) * nc + cc[:, None, None, None]) * width
        + t[None, None, None, :]
    ).reshape(-1)
    grad_wide = grad_t.astype(jnp.float32)
    row_flat = mp_index * rows + lax.iota(jnp.int32, rows)
    diag_val = jnp.sum(jnp.where(perm_cols[:, None] == row_flat[None, :], grad_wide, 0.0), axis=0)
    scale_sum = (jnp.sum(grad_wide * grad_wide, axis=0) - diag_val * diag_val) / (
        2.0 * off_weight
    ) + diag_val * (1.0 + diag_val / 2.0)
    back = jnp.dot(second_perm, grad_t, preferred_element_type=jnp.float32)
    result = (back - first.astype(jnp.float32) * scale_sum[None, :]) * inv_std0
    return result.astype(jnp.bfloat16)


def solution(mesh):
    x, y, c = (4, 8, 2)
    sub = Mesh(mesh.devices.reshape(x, y, c, mesh.devices.shape[1]), DP + ("mp",))
    return jax.shard_map(
        shards,
        mesh=sub,
        in_specs=(P(None, DP, None), P(None, "mp")),
        out_specs=P(DP, "mp"),
        check_vma=False,
    )
```

```python
import jax
import jax.numpy as jnp
from jax import lax
from jax.sharding import Mesh
from jax.sharding import PartitionSpec as P

off_weight = 0.0051
eps = 1e-05
DP = ("x", "y", "c")


def shift(v, axis, n, step):
    return lax.ppermute(v, axis, [(i, (i + step) % n) for i in range(n)])


def direct_gather(v, axis):
    n = lax.axis_size(axis)
    got = {0: v}
    for t in range(1, n):
        got[t] = lax.ppermute(v, axis, [(i, (i - t) % n) for i in range(n)])
    return jnp.stack([got[t] for t in range(n)])


def ring_gather(v, axis):
    n = lax.axis_size(axis)
    if n == 1:
        return v[None]
    right = n // 2
    left = n - 1 - right
    got = {0: v}
    cur = v
    for s in range(1, right + 1):
        cur = shift(cur, axis, n, 1)
        got[n - s] = cur
    cur = v
    for s in range(1, left + 1):
        cur = shift(cur, axis, n, -1)
        got[s] = cur
    return jnp.stack([got[t] for t in range(n)])


def dp_ring_gather(v):
    return ring_gather(ring_gather(direct_gather(v, "x"), "y"), "c")


def combine(mean, m2, count, axis, k):
    n = lax.axis_size(axis)
    pairs = [(i, i ^ k) for i in range(n)]
    other = lax.ppermute(jnp.stack([mean, m2]), axis, pairs)
    other_mean, other_m2 = other[0], other[1]
    delta = other_mean - mean
    new_mean = (mean + other_mean) * 0.5
    new_m2 = (m2 + other_m2) + delta * delta * (count * 0.5)
    return new_mean, new_m2, count * 2


def combine_all(mean, m2, count, axis):
    n = lax.axis_size(axis)
    got = jnp.roll(direct_gather(jnp.stack([mean, m2]), axis), lax.axis_index(axis), axis=0)
    means = [got[j, 0] for j in range(n)]
    m2s = [got[j, 1] for j in range(n)]
    while len(means) > 1:
        new_means, new_m2s = [], []
        for a in range(0, len(means), 2):
            delta = means[a + 1] - means[a]
            new_means.append((means[a] + means[a + 1]) * 0.5)
            new_m2s.append((m2s[a] + m2s[a + 1]) + delta * delta * (count * 0.5))
        means, m2s, count = new_means, new_m2s, count * 2
    return means[0], m2s[0], count


def dp_stats(feats):
    local = feats.shape[1]
    mean = jnp.sum(feats, axis=1, keepdims=True) / local
    dev = feats - mean
    m2 = jnp.sum(dev * dev, axis=1, keepdims=True)
    count = float(local)
    for axis in ("c", "y"):
        k = 1
        while k < lax.axis_size(axis):
            mean, m2, count = combine(mean, m2, count, axis, k)
            k *= 2
    mean, m2, count = combine_all(mean, m2, count, "x")
    return mean, m2 / count


def shards(hidden, proj_weight):
    mp_index = lax.axis_index("mp")
    dp_index = lax.axis_index(DP)
    dp_count = lax.axis_size(DP)
    nx, ny, nc = lax.axis_size("x"), lax.axis_size("y"), lax.axis_size("c")
    ix, iy, ic = lax.axis_index("x"), lax.axis_index("y"), lax.axis_index("c")
    rows = proj_weight.shape[1]
    local = hidden.shape[1]
    total = local * dp_count
    feats = jnp.einsum("vbh,hc->vbc", hidden, proj_weight, preferred_element_type=jnp.float32)
    feats0_all = lax.all_gather(feats[0], DP, axis=0, tiled=True)
    mean0 = jnp.sum(feats0_all, axis=0, keepdims=True) / total
    centered0 = feats0_all - mean0
    var0 = jnp.sum(centered0 * centered0, axis=0, keepdims=True) / total
    first_all = (centered0 / jnp.sqrt(var0 + eps)).astype(jnp.bfloat16)
    first = ((feats[0] - mean0) / jnp.sqrt(var0 + eps)).astype(jnp.bfloat16)
    inv_std0 = 1.0 / jnp.sqrt(var0 + eps)
    mean1, var1 = dp_stats(feats[1:])
    second = ((feats[1] - mean1[0]) / jnp.sqrt(var1[0] + eps)).astype(jnp.bfloat16)
    n_mp = lax.axis_size("mp")
    stacked = lax.all_gather(second, "mp", axis=0)
    second_full = jnp.transpose(stacked, (1, 0, 2)).reshape(local, n_mp * rows)
    width = second_full.shape[1] // dp_count
    chips = lax.all_to_all(second_full, ("x", "y"), split_axis=1, concat_axis=0, tiled=True)
    pc = (lax.iota(jnp.int32, nc)[:, None, None] + ic) % nc
    py = (lax.iota(jnp.int32, ny)[None, :, None] + iy) % ny
    px = (lax.iota(jnp.int32, nx)[None, None, :] + ix) % nx
    src_block = ((px * ny + py) * nc + pc).reshape(-1)
    pick = (src_block[:, None] == lax.iota(jnp.int32, dp_count)[None, :]).astype(jnp.bfloat16)
    second_perm = jnp.einsum(
        "bkt,pk->bpt", second_full.reshape(local, dp_count, width), pick, preferred_element_type=jnp.float32
    ).astype(jnp.bfloat16).reshape(local, dp_count * width)
    chips, second_perm = lax.optimization_barrier((chips, second_perm))
    first_c = lax.dynamic_index_in_dim(first_all.reshape(nx * ny, nc, local, rows), ic, axis=1, keepdims=False)
    part = jnp.einsum(
        "bi,bj->ij", first_c.reshape(total // nc, rows), chips, preferred_element_type=jnp.float32
    )
    mine = lax.dynamic_slice_in_dim(part, ic * width, width, axis=1)
    theirs = lax.dynamic_slice_in_dim(part, (1 - ic) * width, width, axis=1)
    corr = (mine + shift(theirs, "c", nc, 1)) / total
    row_ids = mp_index * rows + lax.iota(jnp.int32, rows)[:, None]
    col_ids = dp_index * width + lax.iota(jnp.int32, width)[None, :]
    grad_block = jnp.where(row_ids == col_ids, 2.0 * (corr - 1.0), 2.0 * off_weight * corr).astype(
        jnp.bfloat16
    )
    grad_t = dp_ring_gather(grad_block.T).reshape(dp_count * width, rows)
    t = lax.iota(jnp.int32, width)
    cc = (lax.iota(jnp.int32, nc) + ic) % nc
    yy = (lax.iota(jnp.int32, ny) + iy) % ny
    xx = (lax.iota(jnp.int32, nx) + ix) % nx
    perm_cols = (
        ((xx[None, None, :, None] * ny + yy[None, :, None, None]) * nc + cc[:, None, None, None]) * width
        + t[None, None, None, :]
    ).reshape(-1)
    grad_wide = grad_t.astype(jnp.float32)
    row_flat = mp_index * rows + lax.iota(jnp.int32, rows)
    diag_val = jnp.sum(jnp.where(perm_cols[:, None] == row_flat[None, :], grad_wide, 0.0), axis=0)
    scale_sum = (jnp.sum(grad_wide * grad_wide, axis=0) - diag_val * diag_val) / (
        2.0 * off_weight
    ) + diag_val * (1.0 + diag_val / 2.0)
    back = jnp.dot(second_perm, grad_t, preferred_element_type=jnp.float32)
    result = (back - first.astype(jnp.float32) * scale_sum[None, :]) * inv_std0
    return result.astype(jnp.bfloat16)


def solution(mesh):
    x, y, c = (4, 8, 2)
    sub = Mesh(mesh.devices.reshape(x, y, c, mesh.devices.shape[1]), DP + ("mp",))
    return jax.shard_map(
        shards,
        mesh=sub,
        in_specs=(P(None, DP, None), P(None, "mp")),
        out_specs=P(DP, "mp"),
        check_vma=False,
    )
```

```python
import jax
import jax.numpy as jnp
from jax import lax
from jax.sharding import Mesh
from jax.sharding import PartitionSpec as P

off_weight = 0.0051
eps = 1e-05
DP = ("x", "y", "c")


def shift(v, axis, n, step):
    return lax.ppermute(v, axis, [(i, (i + step) % n) for i in range(n)])


def direct_gather(v, axis):
    n = lax.axis_size(axis)
    got = {0: v}
    for t in range(1, n):
        got[t] = lax.ppermute(v, axis, [(i, (i - t) % n) for i in range(n)])
    return jnp.stack([got[t] for t in range(n)])


def ring_gather(v, axis):
    n = lax.axis_size(axis)
    if n == 1:
        return v[None]
    right = n // 2
    left = n - 1 - right
    got = {0: v}
    cur = v
    for s in range(1, right + 1):
        cur = shift(cur, axis, n, 1)
        got[n - s] = cur
    cur = v
    for s in range(1, left + 1):
        cur = shift(cur, axis, n, -1)
        got[s] = cur
    return jnp.stack([got[t] for t in range(n)])


def dp_ring_gather(v):
    return ring_gather(ring_gather(direct_gather(v, "x"), "y"), "c")


def combine(mean, m2, count, axis, k):
    n = lax.axis_size(axis)
    pairs = [(i, i ^ k) for i in range(n)]
    other = lax.ppermute(jnp.stack([mean, m2]), axis, pairs)
    other_mean, other_m2 = other[0], other[1]
    delta = other_mean - mean
    new_mean = (mean + other_mean) * 0.5
    new_m2 = (m2 + other_m2) + delta * delta * (count * 0.5)
    return new_mean, new_m2, count * 2


def combine_all(mean, m2, count, axis):
    n = lax.axis_size(axis)
    got = jnp.roll(direct_gather(jnp.stack([mean, m2]), axis), lax.axis_index(axis), axis=0)
    means = [got[j, 0] for j in range(n)]
    m2s = [got[j, 1] for j in range(n)]
    while len(means) > 1:
        new_means, new_m2s = [], []
        for a in range(0, len(means), 2):
            delta = means[a + 1] - means[a]
            new_means.append((means[a] + means[a + 1]) * 0.5)
            new_m2s.append((m2s[a] + m2s[a + 1]) + delta * delta * (count * 0.5))
        means, m2s, count = new_means, new_m2s, count * 2
    return means[0], m2s[0], count


def dp_stats(feats):
    local = feats.shape[1]
    mean = jnp.sum(feats, axis=1, keepdims=True) / local
    dev = feats - mean
    m2 = jnp.sum(dev * dev, axis=1, keepdims=True)
    count = float(local)
    for axis in ("c", "y"):
        k = 1
        while k < lax.axis_size(axis):
            mean, m2, count = combine(mean, m2, count, axis, k)
            k *= 2
    mean, m2, count = combine_all(mean, m2, count, "x")
    return mean, m2 / count


def group_sum(v, group=128):
    part = jnp.sum(v.reshape(v.shape[0] // group, group, v.shape[1]), axis=1)
    return jnp.sum(lax.optimization_barrier(part), axis=0, keepdims=True)


def shards(hidden, proj_weight):
    mp_index = lax.axis_index("mp")
    dp_index = lax.axis_index(DP)
    dp_count = lax.axis_size(DP)
    nx, ny, nc = lax.axis_size("x"), lax.axis_size("y"), lax.axis_size("c")
    ix, iy, ic = lax.axis_index("x"), lax.axis_index("y"), lax.axis_index("c")
    rows = proj_weight.shape[1]
    local = hidden.shape[1]
    total = local * dp_count
    feats = jnp.einsum("vbh,hc->vbc", hidden, proj_weight, preferred_element_type=jnp.float32)
    feats0_all = lax.all_gather(feats[0], DP, axis=0, tiled=True)
    mean0 = group_sum(feats0_all) / total
    centered0 = feats0_all - mean0
    var0 = group_sum(centered0 * centered0) / total
    first_all = (centered0 / jnp.sqrt(var0 + eps)).astype(jnp.bfloat16)
    first = ((feats[0] - mean0) / jnp.sqrt(var0 + eps)).astype(jnp.bfloat16)
    inv_std0 = 1.0 / jnp.sqrt(var0 + eps)
    mean1, var1 = dp_stats(feats[1:])
    second = ((feats[1] - mean1[0]) / jnp.sqrt(var1[0] + eps)).astype(jnp.bfloat16)
    n_mp = lax.axis_size("mp")
    stacked = lax.all_gather(second, "mp", axis=0)
    second_full = jnp.transpose(stacked, (1, 0, 2)).reshape(local, n_mp * rows)
    width = second_full.shape[1] // dp_count
    chips = lax.all_to_all(second_full, ("x", "y"), split_axis=1, concat_axis=0, tiled=True)
    pc = (lax.iota(jnp.int32, nc)[:, None, None] + ic) % nc
    py = (lax.iota(jnp.int32, ny)[None, :, None] + iy) % ny
    px = (lax.iota(jnp.int32, nx)[None, None, :] + ix) % nx
    src_block = ((px * ny + py) * nc + pc).reshape(-1)
    pick = (src_block[:, None] == lax.iota(jnp.int32, dp_count)[None, :]).astype(jnp.bfloat16)
    second_perm = jnp.einsum(
        "bkt,pk->bpt", second_full.reshape(local, dp_count, width), pick, preferred_element_type=jnp.float32
    ).astype(jnp.bfloat16).reshape(local, dp_count * width)
    chips, second_perm = lax.optimization_barrier((chips, second_perm))
    first_c = lax.dynamic_index_in_dim(first_all.reshape(nx * ny, nc, local, rows), ic, axis=1, keepdims=False)
    part = jnp.einsum(
        "bi,bj->ij", first_c.reshape(total // nc, rows), chips, preferred_element_type=jnp.float32
    )
    mine = lax.dynamic_slice_in_dim(part, ic * width, width, axis=1)
    theirs = lax.dynamic_slice_in_dim(part, (1 - ic) * width, width, axis=1)
    corr = (mine + shift(theirs, "c", nc, 1)) / total
    row_ids = mp_index * rows + lax.iota(jnp.int32, rows)[:, None]
    col_ids = dp_index * width + lax.iota(jnp.int32, width)[None, :]
    grad_block = jnp.where(row_ids == col_ids, 2.0 * (corr - 1.0), 2.0 * off_weight * corr).astype(
        jnp.bfloat16
    )
    grad_t = dp_ring_gather(grad_block.T).reshape(dp_count * width, rows)
    t = lax.iota(jnp.int32, width)
    cc = (lax.iota(jnp.int32, nc) + ic) % nc
    yy = (lax.iota(jnp.int32, ny) + iy) % ny
    xx = (lax.iota(jnp.int32, nx) + ix) % nx
    perm_cols = (
        ((xx[None, None, :, None] * ny + yy[None, :, None, None]) * nc + cc[:, None, None, None]) * width
        + t[None, None, None, :]
    ).reshape(-1)
    grad_wide = grad_t.astype(jnp.float32)
    row_flat = mp_index * rows + lax.iota(jnp.int32, rows)
    diag_val = jnp.sum(jnp.where(perm_cols[:, None] == row_flat[None, :], grad_wide, 0.0), axis=0)
    scale_sum = (jnp.sum(grad_wide * grad_wide, axis=0) - diag_val * diag_val) / (
        2.0 * off_weight
    ) + diag_val * (1.0 + diag_val / 2.0)
    back = jnp.dot(second_perm, grad_t, preferred_element_type=jnp.float32)
    result = (back - first.astype(jnp.float32) * scale_sum[None, :]) * inv_std0
    return result.astype(jnp.bfloat16)


def solution(mesh):
    x, y, c = (4, 8, 2)
    sub = Mesh(mesh.devices.reshape(x, y, c, mesh.devices.shape[1]), DP + ("mp",))
    return jax.shard_map(
        shards,
        mesh=sub,
        in_specs=(P(None, DP, None), P(None, "mp")),
        out_specs=P(DP, "mp"),
        check_vma=False,
    )
```
